512 devices in a mesh: fibre: 128 (over x, y_hi, z), seg: 4 (over y_lo, core).
Axes of the slice: x: 4, y: 4 (y_hi: 2, y_lo: 2; y = y_hi * 2 + y_lo), z: 16, core: 2. Of those that a mesh axis runs over, the one named last changes fastest.
Arguments:
- data: bfloat16 [4, 1024, 2048], P('seg', 'fibre')
- sources: int32 [2, 4], replicated, may hold values from 0 to 7
- owners: int32 [2], replicated, may hold values from 0 to 127
Outputs:
- correlations: float32 [2, 4, 1024, 1024], P(None, None, ('fibre', 'seg'))
The draws below stay inside these ranges and needn't reach their ends.
All inputs are finite; a program needn't handle non-finite values.
Results may differ from the reference program's by a relative error of at most 0.0066.
Values may be sent and summed in bfloat16 or wider, within the bound.
No kernel may reach another device: no remote copies, remote signals or barrier semaphores. Data moves between devices by JAX's collectives and lax.ppermute only.
A program may use at most 64 MiB of HBM per device.

```python
import math
import jax
import jax.numpy as jnp
from jax import lax

CH_DEV = 8
L = 2048
BAND = 128
LAGS = 1024
NSRC = 4
STEPS = 2
C = 1024
SEGS = 4
N_FIBRE = 128


def draw_data(key, part):
    key_noise, key_gain, key_colour = jax.random.split(key, 3)
    noise = jax.random.normal(key_noise, (SEGS, C, L + 1), jnp.float32)
    gains = jnp.exp(jax.random.uniform(key_gain, (SEGS, C, 1), jnp.float32, 0.0, math.log(10.0)))
    colour = jax.random.uniform(key_colour, (1, C, 1), jnp.float32, -0.9, 0.9)
    records = gains * (noise[..., 1:] + colour * noise[..., :-1])
    return records.astype(jnp.bfloat16)


def plant(result, stream_key, low, high):
    longest = result.shape.index(max(result.shape))
    spots = []
    for shift in (0, 1):
        where = [jax.random.randint(jax.random.fold_in(stream_key, axis), (), 0, length) for axis, length in enumerate(result.shape)]
        where[longest] = (where[longest] + shift) % result.shape[longest]
        spots.append(tuple(where))
    return result.at[spots[0]].set(low).at[spots[1]].set(high)


def setup_inputs(seed: int = 0) -> dict:
    arg_keys = jax.random.split(jax.random.key(seed), 4)
    data = draw_data(jax.random.fold_in(arg_keys[3], 71), 0)
    sources = plant(jax.random.randint(arg_keys[1], (STEPS, NSRC), 0, CH_DEV), jax.random.fold_in(arg_keys[1], 1), 0, CH_DEV - 1).astype(jnp.int32)
    owners = jax.random.randint(arg_keys[2], (STEPS,), 0, N_FIBRE).astype(jnp.int32)
    return dict(data=data, sources=sources, owners=owners)


def make_tables(length, lags):
    half = length // 2
    times = jnp.arange(length, dtype=jnp.int32)
    freqs = jnp.arange(half, dtype=jnp.int32)
    phase = times[:, None] * freqs[None, :] % length
    angle = phase.astype(jnp.float32) * (2.0 * math.pi / length)
    forward = jnp.concatenate([jnp.cos(angle), -jnp.sin(angle)], axis=1).astype(jnp.bfloat16)
    shifts = jnp.arange(lags, dtype=jnp.int32) - lags // 2 + length
    phase_back = freqs[:, None] * shifts[None, :] % length
    angle_back = phase_back.astype(jnp.float32) * (2.0 * math.pi / length)
    inverse = jnp.concatenate([jnp.cos(angle_back), -jnp.sin(angle_back)], axis=0) * (1.0 / math.sqrt(half))
    return (forward, inverse)

def whiten(spectra, band):
    lead = spectra.shape[:-1]
    width = spectra.shape[-1] // 2
    parts = spectra.reshape(lead + (2, width // band, band))
    power = lax.optimization_barrier(jnp.sum(parts * parts, axis=(-3, -1))) / (2.0 * band)
    scale = lax.rsqrt(power + 1e-06)
    return (parts * scale[..., None, :, None]).reshape(spectra.shape)

def cross_sum(receivers, emitters):
    half = receivers.shape[2] // 2
    rec = receivers.astype(jnp.float32)
    emi = emitters.astype(jnp.float32)
    rec_re, rec_im = (rec[..., :half], rec[..., half:])
    emi_re, emi_im = (emi[..., :half], emi[..., half:])
    real_part = jnp.einsum('sck,snk->nck', rec_re, emi_re) + jnp.einsum('sck,snk->nck', rec_im, emi_im)
    imag_part = jnp.einsum('sck,snk->nck', rec_im, emi_re) - jnp.einsum('sck,snk->nck', rec_re, emi_im)
    return jnp.concatenate([real_part, imag_part], axis=-1)

def correlate(cross, inverse):
    count, chans, width = cross.shape
    flat = jnp.dot(cross.reshape(count * chans, width), inverse, precision=lax.Precision.HIGHEST)
    return flat.reshape(count, chans, inverse.shape[1])

def reference(data, sources, owners):
    forward, inverse = make_tables(L, LAGS)
    spectra = jnp.dot(data.reshape(SEGS * C, L), forward, preferred_element_type=jnp.float32).reshape(SEGS, C, L)
    white = whiten(spectra, BAND).astype(jnp.bfloat16)
    padded = jnp.pad(white.astype(jnp.float32), ((0, 0), (4, 4), (0, 0)))
    total = padded[:, 0:C]
    for offset in range(1, 8):
        total = total + padded[:, offset:offset + C]
    stacked = (total * 0.125).astype(jnp.bfloat16)
    results = []
    for step in range(STEPS):
        channel = (owners[step] * CH_DEV + sources[step]).astype(jnp.int32)
        emitters = jnp.take(white, channel, axis=1)
        results.append(correlate(cross_sum(stacked, emitters), inverse))
    return jnp.stack(results)
```

```python
import math

import jax
import jax.numpy as jnp
from jax import lax
from jax.sharding import PartitionSpec as P

BAND = 128
LAGS = 1024
LOW = 4
HIGH = 3


def radices(count):
    if count == 128:
        return [4, 4, 2, 4]
    out = []
    while count % 4 == 0:
        out.append(4)
        count //= 4
    while count % 2 == 0:
        out.append(2)
        count //= 2
    if count > 1:
        out.append(count)
    return out


def broadcast(block, axis):
    count = lax.axis_size(axis)
    stride = 1
    for radix in radices(count):
        total = block
        for shift in range(1, radix):
            perm = []
            for i in range(count):
                digit = (i // stride) % radix
                perm.append((i, i + ((digit + shift) % radix - digit) * stride))
            total = total + lax.ppermute(block, axis, perm)
        block = total
        stride *= radix
    return block


def gather(block, axis):
    count = lax.axis_size(axis)
    pieces = [block]
    for shift in range(1, count):
        pieces.append(lax.ppermute(block, axis, [(i, (i + shift) % count) for i in range(count)]))
    return jnp.concatenate(pieces, axis=0)


def halo(cells, axis, dim):
    count = lax.axis_size(axis)
    ends = count - 1
    tail = lax.slice_in_dim(cells, cells.shape[dim] - LOW, cells.shape[dim], axis=dim)
    head = lax.slice_in_dim(cells, 0, HIGH, axis=dim)
    return jnp.concatenate(
        [
            lax.ppermute(tail, axis, [(i, i + 1) for i in range(ends)]),
            cells,
            lax.ppermute(head, axis, [(i + 1, i) for i in range(ends)]),
        ],
        axis=dim,
    )


def cos_sin(phase, period):
    angle = phase.astype(jnp.float32) * (2.0 * math.pi / period)
    return jnp.cos(angle), jnp.sin(angle)


def make_forward(length):
    half = length // 2
    lo_count = 64
    hi_count = length // lo_count
    freqs = jnp.arange(half, dtype=jnp.int32)
    hi = jnp.arange(hi_count, dtype=jnp.int32)
    lo = jnp.arange(lo_count, dtype=jnp.int32)
    hi_c, hi_s = cos_sin(hi[:, None] * freqs[None, :] % hi_count, hi_count)
    lo_c, lo_s = cos_sin(lo[:, None] * freqs[None, :] % length, length)
    cos = hi_c[:, None, :] * lo_c[None, :, :] - hi_s[:, None, :] * lo_s[None, :, :]
    sin = hi_s[:, None, :] * lo_c[None, :, :] + hi_c[:, None, :] * lo_s[None, :, :]
    table = jnp.concatenate([cos, -sin], axis=-1)
    return table.reshape(length, length).astype(jnp.bfloat16)


def make_inverse(length, lags):
    half = length // 2
    lo_count = 32
    hi_count = half // lo_count
    period = length // lo_count
    shifts = jnp.arange(lags, dtype=jnp.int32) - lags // 2 + length
    hi = jnp.arange(hi_count, dtype=jnp.int32)
    lo = jnp.arange(lo_count, dtype=jnp.int32)
    hi_c, hi_s = cos_sin(hi[:, None] * shifts[None, :] % period, period)
    lo_c, lo_s = cos_sin(lo[:, None] * shifts[None, :] % length, length)
    cos = hi_c[:, None, :] * lo_c[None, :, :] - hi_s[:, None, :] * lo_s[None, :, :]
    sin = hi_s[:, None, :] * lo_c[None, :, :] + hi_c[:, None, :] * lo_s[None, :, :]
    table = jnp.concatenate([cos.reshape(half, lags), -sin.reshape(half, lags)], axis=0)
    return table * (1.0 / math.sqrt(half))


def whiten(spectra, band):
    lead = spectra.shape[:-1]
    width = spectra.shape[-1] // 2
    parts = spectra.reshape(lead + (2, width // band, band))
    power = jnp.sum(parts * parts, axis=(-3, -1)) / (2.0 * band)
    scale = lax.rsqrt(power + 1e-06)
    return (parts * scale[..., None, :, None]).reshape(spectra.shape)


def cross_sum(receivers, emitters):
    half = receivers.shape[2] // 2
    rec_re, rec_im = (receivers[..., :half], receivers[..., half:])
    emi_re, emi_im = (emitters[..., :half], emitters[..., half:])
    real_part = jnp.einsum("sck,snk->nck", rec_re, emi_re, preferred_element_type=jnp.float32)
    real_part = real_part + jnp.einsum(
        "sck,snk->nck", rec_im, emi_im, preferred_element_type=jnp.float32
    )
    imag_part = jnp.einsum("sck,snk->nck", rec_im, emi_re, preferred_element_type=jnp.float32)
    imag_part = imag_part - jnp.einsum(
        "sck,snk->nck", rec_re, emi_im, preferred_element_type=jnp.float32
    )
    return jnp.concatenate([real_part, imag_part], axis=-1)


def shards(data, sources, owners):
    seg_dev, ch_dev, length = data.shape
    steps, nsrc = sources.shape
    seg_count = lax.axis_size("seg")
    per = ch_dev // seg_count
    selector = (sources[:, :, None] == jnp.arange(ch_dev, dtype=jnp.int32)[None, None, :]).astype(
        jnp.bfloat16
    )
    picked = jnp.einsum("pnc,scf->spnf", selector, data, preferred_element_type=jnp.float32)
    picked = picked.astype(jnp.bfloat16)
    here = lax.axis_index("fibre")
    masked = [
        jnp.where(here == owners[step], picked[:, step], jnp.zeros_like(picked[:, step]))
        for step in range(steps)
    ]
    received = broadcast(jnp.concatenate(masked, axis=1), "fibre")
    window = halo(data, "fibre", 1)
    rows = window.shape[1]
    block = jnp.concatenate([window, received], axis=1)
    block = gather(block, "seg")
    segs = block.shape[0]
    forward = make_forward(length)
    inverse = make_inverse(length, LAGS)
    spectra = jnp.dot(
        block.reshape(segs * block.shape[1], length), forward, preferred_element_type=jnp.float32
    )
    white = whiten(spectra.reshape(block.shape), BAND).astype(jnp.bfloat16)
    chosen = white[:, rows:].reshape(segs, steps, nsrc, length)
    start = lax.axis_index("seg") * per
    part = lax.dynamic_slice_in_dim(white[:, :rows], start, per + LOW + HIGH, axis=1)
    total = part[:, 0:per].astype(jnp.float32)
    for offset in range(1, LOW + HIGH + 1):
        total = total + part[:, offset : offset + per].astype(jnp.float32)
    stacked = (total * 0.125).astype(jnp.bfloat16)
    cross = jnp.stack([cross_sum(stacked, chosen[:, step]) for step in range(steps)])
    flat = jnp.dot(
        cross.reshape(-1, length), inverse, precision=lax.Precision.HIGHEST
    )
    return flat.reshape(steps, nsrc, per, LAGS)


def solution(mesh):
    return jax.shard_map(
        shards,
        mesh=mesh,
        in_specs=(P("seg", "fibre", None), P(), P()),
        out_specs=P(None, None, ("fibre", "seg"), None),
        check_vma=False,
    )
```

```python
import math

import jax
import jax.numpy as jnp
from jax import lax
from jax.sharding import PartitionSpec as P

BAND = 128
LAGS = 1024
LOW = 4
HIGH = 3


def radices(count):
    if count == 128:
        return [4, 4, 2, 4]
    out = []
    while count % 4 == 0:
        out.append(4)
        count //= 4
    while count % 2 == 0:
        out.append(2)
        count //= 2
    if count > 1:
        out.append(count)
    return out


def broadcast(block, axis):
    count = lax.axis_size(axis)
    stride = 1
    for radix in radices(count):
        total = block
        for shift in range(1, radix):
            perm = []
            for i in range(count):
                digit = (i // stride) % radix
                perm.append((i, i + ((digit + shift) % radix - digit) * stride))
            total = total + lax.ppermute(block, axis, perm)
        block = total
        stride *= radix
    return block


def gather(block, axis):
    count = lax.axis_size(axis)
    pieces = [block]
    for shift in range(1, count):
        pieces.append(lax.ppermute(block, axis, [(i, (i + shift) % count) for i in range(count)]))
    return jnp.concatenate(pieces, axis=0)


def halo(cells, axis, dim):
    count = lax.axis_size(axis)
    ends = count - 1
    tail = lax.slice_in_dim(cells, cells.shape[dim] - LOW, cells.shape[dim], axis=dim)
    head = lax.slice_in_dim(cells, 0, HIGH, axis=dim)
    return jnp.concatenate(
        [
            lax.ppermute(tail, axis, [(i, i + 1) for i in range(ends)]),
            cells,
            lax.ppermute(head, axis, [(i + 1, i) for i in range(ends)]),
        ],
        axis=dim,
    )


def cos_sin(phase, period):
    angle = phase.astype(jnp.float32) * (2.0 * math.pi / period)
    return jnp.cos(angle), jnp.sin(angle)


def make_forward(length):
    half = length // 2
    lo_count = 64
    hi_count = length // lo_count
    freqs = jnp.arange(half, dtype=jnp.int32)
    hi = jnp.arange(hi_count, dtype=jnp.int32)
    lo = jnp.arange(lo_count, dtype=jnp.int32)
    hi_c, hi_s = cos_sin(hi[:, None] * freqs[None, :] % hi_count, hi_count)
    lo_c, lo_s = cos_sin(lo[:, None] * freqs[None, :] % length, length)
    cos = hi_c[:, None, :] * lo_c[None, :, :] - hi_s[:, None, :] * lo_s[None, :, :]
    sin = hi_s[:, None, :] * lo_c[None, :, :] + hi_c[:, None, :] * lo_s[None, :, :]
    cos = cos.reshape(length, half).astype(jnp.bfloat16)
    sin = sin.reshape(length, half).astype(jnp.bfloat16)
    return cos, sin


def make_inverse(length, lags):
    half = length // 2
    lo_count = 32
    hi_count = half // lo_count
    period = length // lo_count
    shifts = jnp.arange(lags, dtype=jnp.int32) - lags // 2 + length
    hi = jnp.arange(hi_count, dtype=jnp.int32)
    lo = jnp.arange(lo_count, dtype=jnp.int32)
    hi_c, hi_s = cos_sin(hi[:, None] * shifts[None, :] % period, period)
    lo_c, lo_s = cos_sin(lo[:, None] * shifts[None, :] % length, length)
    cos = hi_c[:, None, :] * lo_c[None, :, :] - hi_s[:, None, :] * lo_s[None, :, :]
    sin = hi_s[:, None, :] * lo_c[None, :, :] + hi_c[:, None, :] * lo_s[None, :, :]
    table = jnp.concatenate([cos.reshape(half, lags), -sin.reshape(half, lags)], axis=0)
    return table * (1.0 / math.sqrt(half))


def whiten(spectra, band):
    lead = spectra.shape[:-1]
    width = spectra.shape[-1] // 2
    parts = spectra.reshape(lead + (2, width // band, band))
    power = jnp.sum(parts * parts, axis=(-3, -1)) / (2.0 * band)
    scale = lax.rsqrt(power + 1e-06)
    return (parts * scale[..., None, :, None]).reshape(spectra.shape)


def cross_sum(receivers, emitters):
    half = receivers.shape[-1] // 2
    rec = receivers.astype(jnp.float32)[:, None, None]
    emi = emitters.astype(jnp.float32)[:, :, :, None]
    rec_re, rec_im = (rec[..., :half], rec[..., half:])
    emi_re, emi_im = (emi[..., :half], emi[..., half:])
    real_part = jnp.sum(rec_re * emi_re, axis=0) + jnp.sum(rec_im * emi_im, axis=0)
    imag_part = jnp.sum(rec_im * emi_re, axis=0) - jnp.sum(rec_re * emi_im, axis=0)
    return jnp.concatenate([real_part, imag_part], axis=-1)


def shards(data, sources, owners):
    seg_dev, ch_dev, length = data.shape
    steps, nsrc = sources.shape
    seg_count = lax.axis_size("seg")
    per = ch_dev // seg_count
    selector = (sources[:, :, None] == jnp.arange(ch_dev, dtype=jnp.int32)[None, None, :]).astype(
        jnp.bfloat16
    )
    picked = jnp.einsum("pnc,scf->spnf", selector, data, preferred_element_type=jnp.float32)
    picked = picked.astype(jnp.bfloat16)
    here = lax.axis_index("fibre")
    masked = [
        jnp.where(here == owners[step], picked[:, step], jnp.zeros_like(picked[:, step]))
        for step in range(steps)
    ]
    received = broadcast(jnp.concatenate(masked, axis=1), "fibre")
    window = halo(data, "fibre", 1)
    rows = window.shape[1]
    block = jnp.concatenate([window, received], axis=1)
    block = gather(block, "seg")
    segs = block.shape[0]
    cos, sin = make_forward(length)
    inverse = make_inverse(length, LAGS)
    flat_rows = block.reshape(segs * block.shape[1], length)
    spectra = jnp.concatenate(
        [
            jnp.dot(flat_rows, cos, preferred_element_type=jnp.float32),
            -jnp.dot(flat_rows, sin, preferred_element_type=jnp.float32),
        ],
        axis=-1,
    )
    white = whiten(spectra.reshape(block.shape), BAND).astype(jnp.bfloat16)
    chosen = white[:, rows:].reshape(segs, steps, nsrc, length)
    start = lax.axis_index("seg") * per
    part = lax.dynamic_slice_in_dim(white[:, :rows], start, per + LOW + HIGH, axis=1)
    total = part[:, 0:per].astype(jnp.float32)
    for offset in range(1, LOW + HIGH + 1):
        total = total + part[:, offset : offset + per].astype(jnp.float32)
    stacked = (total * 0.125).astype(jnp.bfloat16)
    cross = cross_sum(stacked, chosen)
    flat = jnp.dot(cross.reshape(-1, length), inverse, precision=lax.Precision.HIGHEST)
    return flat.reshape(steps, nsrc, per, LAGS)


def solution(mesh):
    return jax.shard_map(
        shards,
        mesh=mesh,
        in_specs=(P("seg", "fibre", None), P(), P()),
        out_specs=P(None, None, ("fibre", "seg"), None),
        check_vma=False,
    )
```

```python
import math

import jax
import jax.numpy as jnp
from jax import lax
from jax.sharding import PartitionSpec as P

BAND = 128
LAGS = 1024
LOW = 4
HIGH = 3


def radices(count):
    if count == 128:
        return [2] * 7
    out = []
    while count % 4 == 0:
        out.append(4)
        count //= 4
    while count % 2 == 0:
        out.append(2)
        count //= 2
    if count > 1:
        out.append(count)
    return out


def broadcast(block, axis):
    count = lax.axis_size(axis)
    stride = 1
    for radix in radices(count):
        total = block
        for shift in range(1, radix):
            perm = []
            for i in range(count):
                digit = (i // stride) % radix
                perm.append((i, i + ((digit + shift) % radix - digit) * stride))
            total = total + lax.ppermute(block, axis, perm)
        block = total
        stride *= radix
    return block


def gather(block, axis):
    count = lax.axis_size(axis)
    pieces = [block]
    for shift in range(1, count):
        pieces.append(lax.ppermute(block, axis, [(i, (i + shift) % count) for i in range(count)]))
    return jnp.concatenate(pieces, axis=0)


def halo(cells, axis, dim):
    count = lax.axis_size(axis)
    ends = count - 1
    tail = lax.slice_in_dim(cells, cells.shape[dim] - LOW, cells.shape[dim], axis=dim)
    head = lax.slice_in_dim(cells, 0, HIGH, axis=dim)
    return jnp.concatenate(
        [
            lax.ppermute(tail, axis, [(i, i + 1) for i in range(ends)]),
            cells,
            lax.ppermute(head, axis, [(i + 1, i) for i in range(ends)]),
        ],
        axis=dim,
    )


def cos_sin(phase, period):
    angle = phase.astype(jnp.float32) * (2.0 * math.pi / period)
    return jnp.cos(angle), jnp.sin(angle)


def make_forward(length):
    half = length // 2
    lo_count = 64
    hi_count = length // lo_count
    freqs = jnp.arange(half, dtype=jnp.int32)
    hi = jnp.arange(hi_count, dtype=jnp.int32)
    lo = jnp.arange(lo_count, dtype=jnp.int32)
    hi_c, hi_s = cos_sin(hi[:, None] * freqs[None, :] % hi_count, hi_count)
    lo_c, lo_s = cos_sin(lo[:, None] * freqs[None, :] % length, length)
    cos = hi_c[:, None, :] * lo_c[None, :, :] - hi_s[:, None, :] * lo_s[None, :, :]
    sin = hi_s[:, None, :] * lo_c[None, :, :] + hi_c[:, None, :] * lo_s[None, :, :]
    cos = cos.reshape(length, half).astype(jnp.bfloat16)
    sin = sin.reshape(length, half).astype(jnp.bfloat16)
    return cos, sin


def make_inverse(length, lags):
    half = length // 2
    lo_count = 32
    hi_count = half // lo_count
    period = length // lo_count
    shifts = jnp.arange(lags, dtype=jnp.int32) - lags // 2 + length
    hi = jnp.arange(hi_count, dtype=jnp.int32)
    lo = jnp.arange(lo_count, dtype=jnp.int32)
    hi_c, hi_s = cos_sin(hi[:, None] * shifts[None, :] % period, period)
    lo_c, lo_s = cos_sin(lo[:, None] * shifts[None, :] % length, length)
    cos = hi_c[:, None, :] * lo_c[None, :, :] - hi_s[:, None, :] * lo_s[None, :, :]
    sin = hi_s[:, None, :] * lo_c[None, :, :] + hi_c[:, None, :] * lo_s[None, :, :]
    table = jnp.concatenate([cos.reshape(half, lags), -sin.reshape(half, lags)], axis=0)
    return table * (1.0 / math.sqrt(half))


def whiten(spectra, band):
    lead = spectra.shape[:-1]
    width = spectra.shape[-1] // 2
    parts = spectra.reshape(lead + (2, width // band, band))
    power = jnp.sum(parts * parts, axis=(-3, -1)) / (2.0 * band)
    scale = lax.rsqrt(power + 1e-06)
    return (parts * scale[..., None, :, None]).reshape(spectra.shape)


def cross_sum(receivers, emitters):
    half = receivers.shape[-1] // 2
    rec = receivers.astype(jnp.float32)[:, None, None]
    emi = emitters.astype(jnp.float32)[:, :, :, None]
    rec_re, rec_im = (rec[..., :half], rec[..., half:])
    emi_re, emi_im = (emi[..., :half], emi[..., half:])
    real_part = jnp.sum(rec_re * emi_re, axis=0) + jnp.sum(rec_im * emi_im, axis=0)
    imag_part = jnp.sum(rec_im * emi_re, axis=0) - jnp.sum(rec_re * emi_im, axis=0)
    return jnp.concatenate([real_part, imag_part], axis=-1)


def shards(data, sources, owners):
    seg_dev, ch_dev, length = data.shape
    steps, nsrc = sources.shape
    seg_count = lax.axis_size("seg")
    per = ch_dev // seg_count
    selector = (sources[:, :, None] == jnp.arange(ch_dev, dtype=jnp.int32)[None, None, :]).astype(
        jnp.bfloat16
    )
    picked = jnp.einsum("pnc,scf->spnf", selector, data, preferred_element_type=jnp.float32)
    picked = picked.astype(jnp.bfloat16)
    here = lax.axis_index("fibre")
    masked = [
        jnp.where(here == owners[step], picked[:, step], jnp.zeros_like(picked[:, step]))
        for step in range(steps)
    ]
    received = broadcast(jnp.concatenate(masked, axis=1), "fibre")
    window = halo(data, "fibre", 1)
    rows = window.shape[1]
    block = jnp.concatenate([window, received], axis=1)
    block = gather(block, "seg")
    segs = block.shape[0]
    cos, sin = make_forward(length)
    inverse = make_inverse(length, LAGS)
    flat_rows = block.reshape(segs * block.shape[1], length)
    spectra = jnp.concatenate(
        [
            jnp.dot(flat_rows, cos, preferred_element_type=jnp.float32),
            -jnp.dot(flat_rows, sin, preferred_element_type=jnp.float32),
        ],
        axis=-1,
    )
    white = whiten(spectra.reshape(block.shape), BAND).astype(jnp.bfloat16)
    chosen = white[:, rows:].reshape(segs, steps, nsrc, length)
    start = lax.axis_index("seg") * per
    part = lax.dynamic_slice_in_dim(white[:, :rows], start, per + LOW + HIGH, axis=1)
    total = part[:, 0:per].astype(jnp.float32)
    for offset in range(1, LOW + HIGH + 1):
        total = total + part[:, offset : offset + per].astype(jnp.float32)
    stacked = (total * 0.125).astype(jnp.bfloat16)
    cross = cross_sum(stacked, chosen)
    flat = jnp.dot(cross.reshape(-1, length), inverse, precision=lax.Precision.HIGH)
    return flat.reshape(steps, nsrc, per, LAGS)


def solution(mesh):
    return jax.shard_map(
        shards,
        mesh=mesh,
        in_specs=(P("seg", "fibre", None), P(), P()),
        out_specs=P(None, None, ("fibre", "seg"), None),
        check_vma=False,
    )
```

```python
import math

import jax
import jax.numpy as jnp
from jax import lax
from jax.sharding import PartitionSpec as P

BAND = 128
LAGS = 1024
LOW = 4
HIGH = 3


def radices(count):
    if count == 128:
        return [2] * 7
    out = []
    while count % 4 == 0:
        out.append(4)
        count //= 4
    while count % 2 == 0:
        out.append(2)
        count //= 2
    if count > 1:
        out.append(count)
    return out


def broadcast(block, axis):
    count = lax.axis_size(axis)
    stride = 1
    for radix in radices(count):
        total = block
        for shift in range(1, radix):
            perm = []
            for i in range(count):
                digit = (i // stride) % radix
                perm.append((i, i + ((digit + shift) % radix - digit) * stride))
            total = total + lax.ppermute(block, axis, perm)
        block = total
        stride *= radix
    return block


def gather(block, axis):
    count = lax.axis_size(axis)
    pieces = [block]
    for shift in range(1, count):
        pieces.append(lax.ppermute(block, axis, [(i, (i + shift) % count) for i in range(count)]))
    return jnp.concatenate(pieces, axis=0)


def halo(cells, axis, dim):
    count = lax.axis_size(axis)
    ends = count - 1
    tail = lax.slice_in_dim(cells, cells.shape[dim] - LOW, cells.shape[dim], axis=dim)
    head = lax.slice_in_dim(cells, 0, HIGH, axis=dim)
    return jnp.concatenate(
        [
            lax.ppermute(tail, axis, [(i, i + 1) for i in range(ends)]),
            cells,
            lax.ppermute(head, axis, [(i + 1, i) for i in range(ends)]),
        ],
        axis=dim,
    )


def cos_sin(phase, period):
    angle = phase.astype(jnp.float32) * (2.0 * math.pi / period)
    return jnp.cos(angle), jnp.sin(angle)


def make_forward(length):
    half = length // 2
    lo_count = 64
    hi_count = length // lo_count
    freqs = jnp.arange(half, dtype=jnp.int32)
    hi = jnp.arange(hi_count, dtype=jnp.int32)
    lo = jnp.arange(lo_count, dtype=jnp.int32)
    hi_c, hi_s = cos_sin(hi[:, None] * freqs[None, :] % hi_count, hi_count)
    lo_c, lo_s = cos_sin(lo[:, None] * freqs[None, :] % length, length)
    cos = hi_c[:, None, :] * lo_c[None, :, :] - hi_s[:, None, :] * lo_s[None, :, :]
    sin = hi_s[:, None, :] * lo_c[None, :, :] + hi_c[:, None, :] * lo_s[None, :, :]
    cos = cos.reshape(length, half).astype(jnp.bfloat16)
    sin = sin.reshape(length, half).astype(jnp.bfloat16)
    return cos, sin


def make_inverse(length, lags):
    half = length // 2
    lo_count = 32
    hi_count = half // lo_count
    period = length // lo_count
    shifts = jnp.arange(lags, dtype=jnp.int32) - lags // 2 + length
    hi = jnp.arange(hi_count, dtype=jnp.int32)
    lo = jnp.arange(lo_count, dtype=jnp.int32)
    hi_c, hi_s = cos_sin(hi[:, None] * shifts[None, :] % period, period)
    lo_c, lo_s = cos_sin(lo[:, None] * shifts[None, :] % length, length)
    cos = hi_c[:, None, :] * lo_c[None, :, :] - hi_s[:, None, :] * lo_s[None, :, :]
    sin = hi_s[:, None, :] * lo_c[None, :, :] + hi_c[:, None, :] * lo_s[None, :, :]
    table = jnp.concatenate([cos.reshape(half, lags), -sin.reshape(half, lags)], axis=0)
    return table * (1.0 / math.sqrt(half))


def whiten(spectra, band):
    lead = spectra.shape[:-1]
    width = spectra.shape[-1] // 2
    parts = spectra.reshape(lead + (2, width // band, band))
    power = jnp.sum(parts * parts, axis=(-3, -1)) / (2.0 * band)
    scale = lax.rsqrt(power + 1e-06)
    return (parts * scale[..., None, :, None]).reshape(spectra.shape)


def cross_sum(receivers, emitters):
    half = receivers.shape[-1] // 2
    rec = receivers.astype(jnp.float32)[:, None, None]
    emi = emitters.astype(jnp.float32)[:, :, :, None]
    rec_re, rec_im = (rec[..., :half], rec[..., half:])
    emi_re, emi_im = (emi[..., :half], emi[..., half:])
    real_part = jnp.sum(rec_re * emi_re, axis=0) + jnp.sum(rec_im * emi_im, axis=0)
    imag_part = jnp.sum(rec_im * emi_re, axis=0) - jnp.sum(rec_re * emi_im, axis=0)
    return jnp.concatenate([real_part, imag_part], axis=-1)


def shards(data, sources, owners):
    seg_dev, ch_dev, length = data.shape
    steps, nsrc = sources.shape
    seg_count = lax.axis_size("seg")
    per = ch_dev // seg_count
    selector = (sources[:, :, None] == jnp.arange(ch_dev, dtype=jnp.int32)[None, None, :]).astype(
        jnp.bfloat16
    )
    picked = jnp.einsum("pnc,scf->spnf", selector, data, preferred_element_type=jnp.float32)
    picked = picked.astype(jnp.bfloat16)
    here = lax.axis_index("fibre")
    masked = [
        jnp.where(here == owners[step], picked[:, step], jnp.zeros_like(picked[:, step]))
        for step in range(steps)
    ]
    received = broadcast(jnp.concatenate(masked, axis=1), "fibre")
    window = gather(halo(data, "fibre", 1), "seg")
    chosen = gather(received, "seg")
    segs, rows, _ = window.shape
    cos, sin = make_forward(length)
    inverse = make_inverse(length, LAGS)

    def transform(block):
        flat_rows = block.reshape(-1, length)
        spectra = jnp.concatenate(
            [
                jnp.dot(flat_rows, cos, preferred_element_type=jnp.float32),
                -jnp.dot(flat_rows, sin, preferred_element_type=jnp.float32),
            ],
            axis=-1,
        )
        return whiten(spectra.reshape(block.shape), BAND).astype(jnp.bfloat16)

    white = transform(window)
    start = lax.axis_index("seg") * per
    part = lax.dynamic_slice_in_dim(white, start, per + LOW + HIGH, axis=1)
    total = part[:, 0:per].astype(jnp.float32)
    for offset in range(1, LOW + HIGH + 1):
        total = total + part[:, offset : offset + per].astype(jnp.float32)
    stacked = (total * 0.125).astype(jnp.bfloat16)
    emitters = transform(chosen).reshape(segs, steps, nsrc, length)
    cross = cross_sum(stacked, emitters)
    flat = lax.dot_general(
        inverse,
        cross.reshape(-1, length),
        (((0,), (1,)), ((), ())),
        precision=lax.Precision.HIGH,
    ).T
    return flat.reshape(steps, nsrc, per, LAGS)


def solution(mesh):
    return jax.shard_map(
        shards,
        mesh=mesh,
        in_specs=(P("seg", "fibre", None), P(), P()),
        out_specs=P(None, None, ("fibre", "seg"), None),
        check_vma=False,
    )
```

```python
import math

import jax
import jax.numpy as jnp
from jax import lax
from jax.sharding import PartitionSpec as P

BAND = 128
LAGS = 1024
LOW = 4
HIGH = 3


def radices(count):
    if count == 128:
        return [2] * 7
    out = []
    while count % 4 == 0:
        out.append(4)
        count //= 4
    while count % 2 == 0:
        out.append(2)
        count //= 2
    if count > 1:
        out.append(count)
    return out


def broadcast(block, axis):
    count = lax.axis_size(axis)
    stride = 1
    for radix in radices(count):
        total = block
        for shift in range(1, radix):
            perm = []
            for i in range(count):
                digit = (i // stride) % radix
                perm.append((i, i + ((digit + shift) % radix - digit) * stride))
            total = total + lax.ppermute(block, axis, perm)
        block = total
        stride *= radix
    return block


def gather(block, axis):
    count = lax.axis_size(axis)
    stride = 1
    while stride < count:
        partner = lax.ppermute(block, axis, [(i, i ^ stride) for i in range(count)])
        block = jnp.concatenate([block, partner], axis=0)
        stride *= 2
    return block


def halo(cells, axis, dim):
    count = lax.axis_size(axis)
    ends = count - 1
    tail = lax.slice_in_dim(cells, cells.shape[dim] - LOW, cells.shape[dim], axis=dim)
    head = lax.slice_in_dim(cells, 0, HIGH, axis=dim)
    return jnp.concatenate(
        [
            lax.ppermute(tail, axis, [(i, i + 1) for i in range(ends)]),
            cells,
            lax.ppermute(head, axis, [(i + 1, i) for i in range(ends)]),
        ],
        axis=dim,
    )


def cos_sin(phase, period):
    angle = phase.astype(jnp.float32) * (2.0 * math.pi / period)
    return jnp.cos(angle), jnp.sin(angle)


def make_forward(length):
    half = length // 2
    lo_count = 64
    hi_count = length // lo_count
    freqs = jnp.arange(half, dtype=jnp.int32)
    hi = jnp.arange(hi_count, dtype=jnp.int32)
    lo = jnp.arange(lo_count, dtype=jnp.int32)
    hi_c, hi_s = cos_sin(hi[:, None] * freqs[None, :] % hi_count, hi_count)
    lo_c, lo_s = cos_sin(lo[:, None] * freqs[None, :] % length, length)
    cos = hi_c[:, None, :] * lo_c[None, :, :] - hi_s[:, None, :] * lo_s[None, :, :]
    sin = hi_s[:, None, :] * lo_c[None, :, :] + hi_c[:, None, :] * lo_s[None, :, :]
    cos = cos.reshape(length, half).astype(jnp.bfloat16)
    sin = sin.reshape(length, half).astype(jnp.bfloat16)
    return cos, sin


def make_inverse(length, lags):
    half = length // 2
    lo_count = 32
    hi_count = half // lo_count
    period = length // lo_count
    shifts = jnp.arange(lags, dtype=jnp.int32) - lags // 2 + length
    hi = jnp.arange(hi_count, dtype=jnp.int32)
    lo = jnp.arange(lo_count, dtype=jnp.int32)
    hi_c, hi_s = cos_sin(hi[:, None] * shifts[None, :] % period, period)
    lo_c, lo_s = cos_sin(lo[:, None] * shifts[None, :] % length, length)
    cos = hi_c[:, None, :] * lo_c[None, :, :] - hi_s[:, None, :] * lo_s[None, :, :]
    sin = hi_s[:, None, :] * lo_c[None, :, :] + hi_c[:, None, :] * lo_s[None, :, :]
    table = jnp.concatenate([cos.reshape(half, lags), -sin.reshape(half, lags)], axis=0)
    return table * (1.0 / math.sqrt(half))


def whiten(spectra, band):
    lead = spectra.shape[:-1]
    width = spectra.shape[-1] // 2
    parts = spectra.reshape(lead + (2, width // band, band))
    power = jnp.sum(parts * parts, axis=(-3, -1)) / (2.0 * band)
    scale = lax.rsqrt(power + 1e-06)
    return (parts * scale[..., None, :, None]).reshape(spectra.shape)


def cross_sum(receivers, emitters):
    half = receivers.shape[-1] // 2
    rec = receivers.astype(jnp.float32)[:, None, None]
    emi = emitters.astype(jnp.float32)[:, :, :, None]
    rec_re, rec_im = (rec[..., :half], rec[..., half:])
    emi_re, emi_im = (emi[..., :half], emi[..., half:])
    real_part = jnp.sum(rec_re * emi_re, axis=0) + jnp.sum(rec_im * emi_im, axis=0)
    imag_part = jnp.sum(rec_im * emi_re, axis=0) - jnp.sum(rec_re * emi_im, axis=0)
    return jnp.concatenate([real_part, imag_part], axis=-1)


def shards(data, sources, owners):
    seg_dev, ch_dev, length = data.shape
    steps, nsrc = sources.shape
    seg_count = lax.axis_size("seg")
    per = ch_dev // seg_count
    here = lax.axis_index("fibre")
    channels = jnp.arange(ch_dev, dtype=jnp.int32)
    keep = (sources[:, :, None] == channels[None, None, :]) & (here == owners)[:, None, None]
    picked = jnp.sum(
        jnp.where(keep.reshape(1, steps * nsrc, ch_dev, 1), data[:, None], jnp.zeros_like(data[:, None])),
        axis=2,
    )
    received = broadcast(picked, "fibre")
    window = halo(data, "fibre", 1)
    rows = window.shape[1]
    block = jnp.concatenate([window, received], axis=1)
    block = gather(block, "seg")
    segs = block.shape[0]
    cos, sin = make_forward(length)
    inverse = make_inverse(length, LAGS)
    flat_rows = block.reshape(segs * block.shape[1], length)
    spectra = jnp.concatenate(
        [
            jnp.dot(flat_rows, cos, preferred_element_type=jnp.float32),
            -jnp.dot(flat_rows, sin, preferred_element_type=jnp.float32),
        ],
        axis=-1,
    )
    white = whiten(spectra.reshape(block.shape), BAND).astype(jnp.bfloat16)
    chosen = white[:, rows:].reshape(segs, steps, nsrc, length)
    start = lax.axis_index("seg") * per
    part = lax.dynamic_slice_in_dim(white[:, :rows], start, per + LOW + HIGH, axis=1)
    total = part[:, 0:per].astype(jnp.float32)
    for offset in range(1, LOW + HIGH + 1):
        total = total + part[:, offset : offset + per].astype(jnp.float32)
    stacked = (total * 0.125).astype(jnp.bfloat16)
    cross = cross_sum(stacked, chosen)
    flat = jnp.dot(cross.reshape(-1, length), inverse, precision=lax.Precision.HIGH)
    return flat.reshape(steps, nsrc, per, LAGS)


def solution(mesh):
    return jax.shard_map(
        shards,
        mesh=mesh,
        in_specs=(P("seg", "fibre", None), P(), P()),
        out_specs=P(None, None, ("fibre", "seg"), None),
        check_vma=False,
    )
```

```python
import math

import jax
import jax.numpy as jnp
from jax import lax
from jax.sharding import PartitionSpec as P

BAND = 128
LAGS = 1024
LOW = 4
HIGH = 3


def radices(count):
    if count == 128:
        return [2] * 7
    out = []
    while count % 4 == 0:
        out.append(4)
        count //= 4
    while count % 2 == 0:
        out.append(2)
        count //= 2
    if count > 1:
        out.append(count)
    return out


def broadcast(block, axis):
    count = lax.axis_size(axis)
    stride = 1
    for radix in radices(count):
        total = block
        for shift in range(1, radix):
            perm = []
            for i in range(count):
                digit = (i // stride) % radix
                perm.append((i, i + ((digit + shift) % radix - digit) * stride))
            total = total + lax.ppermute(block, axis, perm)
        block = total
        stride *= radix
    return block


def gather(block, axis):
    count = lax.axis_size(axis)
    stride = 1
    while stride < count:
        partner = lax.ppermute(block, axis, [(i, i ^ stride) for i in range(count)])
        block = jnp.concatenate([block, partner], axis=0)
        stride *= 2
    return block


def halo(cells, axis, dim):
    count = lax.axis_size(axis)
    ends = count - 1
    tail = lax.slice_in_dim(cells, cells.shape[dim] - LOW, cells.shape[dim], axis=dim)
    head = lax.slice_in_dim(cells, 0, HIGH, axis=dim)
    return jnp.concatenate(
        [
            lax.ppermute(tail, axis, [(i, i + 1) for i in range(ends)]),
            cells,
            lax.ppermute(head, axis, [(i + 1, i) for i in range(ends)]),
        ],
        axis=dim,
    )


def cos_sin(phase, period):
    angle = phase.astype(jnp.float32) * (2.0 * math.pi / period)
    return jnp.cos(angle), jnp.sin(angle)


def make_forward(length):
    half = length // 2
    lo_count = 64
    hi_count = length // lo_count
    freqs = jnp.arange(half, dtype=jnp.int32)
    hi = jnp.arange(hi_count, dtype=jnp.int32)
    lo = jnp.arange(lo_count, dtype=jnp.int32)
    hi_c, hi_s = cos_sin(hi[:, None] * freqs[None, :] % hi_count, hi_count)
    lo_c, lo_s = cos_sin(lo[:, None] * freqs[None, :] % length, length)
    cos = hi_c[:, None, :] * lo_c[None, :, :] - hi_s[:, None, :] * lo_s[None, :, :]
    sin = hi_s[:, None, :] * lo_c[None, :, :] + hi_c[:, None, :] * lo_s[None, :, :]
    cos = cos.reshape(length, half).astype(jnp.bfloat16)
    sin = sin.reshape(length, half).astype(jnp.bfloat16)
    return cos, sin


def inverse_transform(cross, lags):
    count, length = cross.shape
    half = length // 2
    inner = 32
    outer = half // inner
    period = length // inner
    turns = lags // period
    shift = length - lags // 2
    hi = jnp.arange(outer, dtype=jnp.int32)
    lo = jnp.arange(inner, dtype=jnp.int32)
    cols = jnp.arange(period, dtype=jnp.int32)
    laps = jnp.arange(turns, dtype=jnp.int32)
    e_c, e_s = cos_sin(hi[:, None] * cols[None, :] % period, period)
    first = jnp.concatenate(
        [jnp.concatenate([e_c, e_s], axis=1), jnp.concatenate([-e_s, e_c], axis=1)], axis=0
    )
    parts = jnp.concatenate(
        [cross[:, :half].reshape(count, outer, inner), cross[:, half:].reshape(count, outer, inner)],
        axis=1,
    )
    spun = jnp.einsum("rab,am->rbm", parts, first, precision=lax.Precision.HIGHEST)
    u_re, u_im = spun[..., :period], spun[..., period:]
    t_c, t_s = cos_sin(lo[:, None] * (cols[None, :] + shift) % length, length)
    twisted = jnp.concatenate([u_re * t_c - u_im * t_s, u_re * t_s + u_im * t_c], axis=1)
    f_c, f_s = cos_sin(lo[:, None] * laps[None, :] % inner, inner)
    second = jnp.concatenate([f_c, -f_s], axis=0)
    out = jnp.einsum("rbm,bq->rqm", twisted, second, precision=lax.Precision.HIGHEST)
    return out.reshape(count, lags) * (1.0 / math.sqrt(half))


def whiten(spectra, band):
    lead = spectra.shape[:-1]
    width = spectra.shape[-1] // 2
    parts = spectra.reshape(lead + (2, width // band, band))
    power = jnp.sum(parts * parts, axis=(-3, -1)) / (2.0 * band)
    scale = lax.rsqrt(power + 1e-06)
    return (parts * scale[..., None, :, None]).reshape(spectra.shape)


def cross_sum(receivers, emitters):
    half = receivers.shape[-1] // 2
    rec = receivers.astype(jnp.float32)[:, None, None]
    emi = emitters.astype(jnp.float32)[:, :, :, None]
    rec_re, rec_im = (rec[..., :half], rec[..., half:])
    emi_re, emi_im = (emi[..., :half], emi[..., half:])
    real_part = jnp.sum(rec_re * emi_re, axis=0) + jnp.sum(rec_im * emi_im, axis=0)
    imag_part = jnp.sum(rec_im * emi_re, axis=0) - jnp.sum(rec_re * emi_im, axis=0)
    return jnp.concatenate([real_part, imag_part], axis=-1)


def shards(data, sources, owners):
    seg_dev, ch_dev, length = data.shape
    steps, nsrc = sources.shape
    seg_count = lax.axis_size("seg")
    per = ch_dev // seg_count
    here = lax.axis_index("fibre")
    channels = jnp.arange(ch_dev, dtype=jnp.int32)
    keep = (sources[:, :, None] == channels[None, None, :]) & (here == owners)[:, None, None]
    picked = jnp.sum(
        jnp.where(keep.reshape(1, steps * nsrc, ch_dev, 1), data[:, None], jnp.zeros_like(data[:, None])),
        axis=2,
    )
    received = broadcast(picked, "fibre")
    window = halo(data, "fibre", 1)
    rows = window.shape[1]
    block = jnp.concatenate([window, received], axis=1)
    block = gather(block, "seg")
    segs = block.shape[0]
    cos, sin = make_forward(length)
    flat_rows = block.reshape(segs * block.shape[1], length)
    spectra = jnp.concatenate(
        [
            jnp.dot(flat_rows, cos, preferred_element_type=jnp.float32),
            -jnp.dot(flat_rows, sin, preferred_element_type=jnp.float32),
        ],
        axis=-1,
    )
    white = whiten(spectra.reshape(block.shape), BAND).astype(jnp.bfloat16)
    chosen = white[:, rows:].reshape(segs, steps, nsrc, length)
    start = lax.axis_index("seg") * per
    part = lax.dynamic_slice_in_dim(white[:, :rows], start, per + LOW + HIGH, axis=1)
    total = part[:, 0:per].astype(jnp.float32)
    for offset in range(1, LOW + HIGH + 1):
        total = total + part[:, offset : offset + per].astype(jnp.float32)
    stacked = (total * 0.125).astype(jnp.bfloat16)
    cross = cross_sum(stacked, chosen)
    flat = inverse_transform(cross.reshape(-1, length), LAGS)
    return flat.reshape(steps, nsrc, per, LAGS)


def solution(mesh):
    return jax.shard_map(
        shards,
        mesh=mesh,
        in_specs=(P("seg", "fibre", None), P(), P()),
        out_specs=P(None, None, ("fibre", "seg"), None),
        check_vma=False,
    )
```

```python
import math

import jax
import jax.numpy as jnp
from jax import lax
from jax.sharding import PartitionSpec as P

BAND = 128
LAGS = 1024
LOW = 4
HIGH = 3


def radices(count):
    if count == 64:
        return [2] * 6
    out = []
    while count % 4 == 0:
        out.append(4)
        count //= 4
    while count % 2 == 0:
        out.append(2)
        count //= 2
    if count > 1:
        out.append(count)
    return out


def broadcast(block, axis, rider):
    count = lax.axis_size(axis)
    width = block.shape[1]
    both = lax.ppermute(jnp.concatenate([block, rider], axis=1), axis, [(i, i ^ 1) for i in range(count)])
    block = block + both[:, :width]
    carried = both[:, width:]
    stride = 2
    for radix in radices(count // 2):
        total = block
        for shift in range(1, radix):
            perm = []
            for i in range(count):
                digit = (i // stride) % radix
                perm.append((i, i + ((digit + shift) % radix - digit) * stride))
            total = total + lax.ppermute(block, axis, perm)
        block = total
        stride *= radix
    return block, carried


def gather(block, axis):
    count = lax.axis_size(axis)
    stride = 1
    while stride < count:
        partner = lax.ppermute(block, axis, [(i, i ^ stride) for i in range(count)])
        block = jnp.concatenate([block, partner], axis=0)
        stride *= 2
    return block


def edges(cells, axis):
    count = lax.axis_size(axis)
    odd = lax.axis_index(axis) % 2 == 1
    rows = cells.shape[1]
    tail = lax.slice_in_dim(cells, rows - LOW, rows, axis=1)
    head = jnp.pad(lax.slice_in_dim(cells, 0, HIGH, axis=1), ((0, 0), (0, LOW - HIGH), (0, 0)))
    rider = jnp.where(odd, head, tail)
    other = jnp.where(odd, tail, head)
    perm = [(i, i + 1) if i % 2 else (i, i - 1) for i in range(count)]
    perm = [(i, j) for i, j in perm if 0 <= j < count]
    return rider, lax.ppermute(other, axis, perm), odd


def halo(cells, near, far, odd):
    lower = jnp.where(odd, near, far)
    upper = jnp.where(odd, far, near)[:, :HIGH]
    return jnp.concatenate([lower, cells, upper], axis=1)


def cos_sin(phase, period):
    angle = phase.astype(jnp.float32) * (2.0 * math.pi / period)
    return jnp.cos(angle), jnp.sin(angle)


def make_forward(length):
    half = length // 2
    lo_count = 64
    hi_count = length // lo_count
    freqs = jnp.arange(half, dtype=jnp.int32)
    hi = jnp.arange(hi_count, dtype=jnp.int32)
    lo = jnp.arange(lo_count, dtype=jnp.int32)
    hi_c, hi_s = cos_sin(hi[:, None] * freqs[None, :] % hi_count, hi_count)
    lo_c, lo_s = cos_sin(lo[:, None] * freqs[None, :] % length, length)
    cos = hi_c[:, None, :] * lo_c[None, :, :] - hi_s[:, None, :] * lo_s[None, :, :]
    sin = hi_s[:, None, :] * lo_c[None, :, :] + hi_c[:, None, :] * lo_s[None, :, :]
    cos = cos.reshape(length, half).astype(jnp.bfloat16)
    sin = sin.reshape(length, half).astype(jnp.bfloat16)
    return cos, sin


def inverse_transform(cross, lags):
    count, length = cross.shape
    half = length // 2
    inner = 32
    outer = half // inner
    period = length // inner
    turns = lags // period
    shift = length - lags // 2
    hi = jnp.arange(outer, dtype=jnp.int32)
    lo = jnp.arange(inner, dtype=jnp.int32)
    cols = jnp.arange(period, dtype=jnp.int32)
    laps = jnp.arange(turns, dtype=jnp.int32)
    e_c, e_s = cos_sin(hi[:, None] * cols[None, :] % period, period)
    first = jnp.concatenate(
        [jnp.concatenate([e_c, e_s], axis=1), jnp.concatenate([-e_s, e_c], axis=1)], axis=0
    )
    parts = jnp.concatenate(
        [cross[:, :half].reshape(count, outer, inner), cross[:, half:].reshape(count, outer, inner)],
        axis=1,
    )
    spun = jnp.einsum("rab,am->rbm", parts, first, precision=lax.Precision.HIGHEST)
    u_re, u_im = spun[..., :period], spun[..., period:]
    t_c, t_s = cos_sin(lo[:, None] * (cols[None, :] + shift) % length, length)
    twisted = jnp.concatenate([u_re * t_c - u_im * t_s, u_re * t_s + u_im * t_c], axis=1)
    f_c, f_s = cos_sin(lo[:, None] * laps[None, :] % inner, inner)
    second = jnp.concatenate([f_c, -f_s], axis=0)
    out = jnp.einsum("rbm,bq->rqm", twisted, second, precision=lax.Precision.HIGHEST)
    return out.reshape(count, lags) * (1.0 / math.sqrt(half))


def whiten(spectra, band):
    lead = spectra.shape[:-1]
    width = spectra.shape[-1] // 2
    parts = spectra.reshape(lead + (2, width // band, band))
    power = jnp.sum(parts * parts, axis=(-3, -1)) / (2.0 * band)
    scale = lax.rsqrt(power + 1e-06)
    return (parts * scale[..., None, :, None]).reshape(spectra.shape)


def cross_sum(receivers, emitters):
    half = receivers.shape[-1] // 2
    rec = receivers.astype(jnp.float32)[:, None, None]
    emi = emitters.astype(jnp.float32)[:, :, :, None]
    rec_re, rec_im = (rec[..., :half], rec[..., half:])
    emi_re, emi_im = (emi[..., :half], emi[..., half:])
    real_part = jnp.sum(rec_re * emi_re, axis=0) + jnp.sum(rec_im * emi_im, axis=0)
    imag_part = jnp.sum(rec_im * emi_re, axis=0) - jnp.sum(rec_re * emi_im, axis=0)
    return jnp.concatenate([real_part, imag_part], axis=-1)


def shards(data, sources, owners):
    seg_dev, ch_dev, length = data.shape
    steps, nsrc = sources.shape
    seg_count = lax.axis_size("seg")
    per = ch_dev // seg_count
    here = lax.axis_index("fibre")
    channels = jnp.arange(ch_dev, dtype=jnp.int32)
    keep = (sources[:, :, None] == channels[None, None, :]) & (here == owners)[:, None, None]
    picked = jnp.sum(
        jnp.where(keep.reshape(1, steps * nsrc, ch_dev, 1), data[:, None], jnp.zeros_like(data[:, None])),
        axis=2,
    )
    rider, far, odd = edges(data, "fibre")
    received, near = broadcast(picked, "fibre", rider)
    window = halo(data, near, far, odd)
    rows = window.shape[1]
    block = jnp.concatenate([window, received], axis=1)
    block = gather(block, "seg")
    segs = block.shape[0]
    cos, sin = make_forward(length)
    flat_rows = block.reshape(segs * block.shape[1], length)
    spectra = jnp.concatenate(
        [
            jnp.dot(flat_rows, cos, preferred_element_type=jnp.float32),
            -jnp.dot(flat_rows, sin, preferred_element_type=jnp.float32),
        ],
        axis=-1,
    )
    white = whiten(spectra.reshape(block.shape), BAND).astype(jnp.bfloat16)
    chosen = white[:, rows:].reshape(segs, steps, nsrc, length)
    start = lax.axis_index("seg") * per
    part = lax.dynamic_slice_in_dim(white[:, :rows], start, per + LOW + HIGH, axis=1)
    total = part[:, 0:per].astype(jnp.float32)
    for offset in range(1, LOW + HIGH + 1):
        total = total + part[:, offset : offset + per].astype(jnp.float32)
    stacked = (total * 0.125).astype(jnp.bfloat16)
    cross = cross_sum(stacked, chosen)
    flat = inverse_transform(cross.reshape(-1, length), LAGS)
    return flat.reshape(steps, nsrc, per, LAGS)


def solution(mesh):
    return jax.shard_map(
        shards,
        mesh=mesh,
        in_specs=(P("seg", "fibre", None), P(), P()),
        out_specs=P(None, None, ("fibre", "seg"), None),
        check_vma=False,
    )
```

```python
import math

import jax
import jax.numpy as jnp
from jax import lax
from jax.sharding import PartitionSpec as P

BAND = 128
LAGS = 1024
LOW = 4
HIGH = 3


def radices(count):
    if count == 64:
        return [2] * 6
    out = []
    while count % 4 == 0:
        out.append(4)
        count //= 4
    while count % 2 == 0:
        out.append(2)
        count //= 2
    if count > 1:
        out.append(count)
    return out


def broadcast(block, axis, rider):
    count = lax.axis_size(axis)
    width = block.shape[1]
    both = lax.ppermute(jnp.concatenate([block, rider], axis=1), axis, [(i, i ^ 1) for i in range(count)])
    block = block + both[:, :width]
    carried = both[:, width:]
    stride = 2
    for radix in radices(count // 2):
        total = block
        for shift in range(1, radix):
            perm = []
            for i in range(count):
                digit = (i // stride) % radix
                perm.append((i, i + ((digit + shift) % radix - digit) * stride))
            total = total + lax.ppermute(block, axis, perm)
        block = total
        stride *= radix
    return block, carried


def gather(block, axis):
    count = lax.axis_size(axis)
    stride = count // 2
    while stride >= 1:
        partner = lax.ppermute(block, axis, [(i, i ^ stride) for i in range(count)])
        block = jnp.concatenate([block, partner], axis=0)
        stride //= 2
    return block


def edges(cells, axis):
    count = lax.axis_size(axis)
    odd = lax.axis_index(axis) % 2 == 1
    rows = cells.shape[1]
    tail = lax.slice_in_dim(cells, rows - LOW, rows, axis=1)
    head = jnp.pad(lax.slice_in_dim(cells, 0, HIGH, axis=1), ((0, 0), (0, LOW - HIGH), (0, 0)))
    rider = jnp.where(odd, head, tail)
    other = jnp.where(odd, tail, head)
    perm = [(i, i + 1) if i % 2 else (i, i - 1) for i in range(count)]
    perm = [(i, j) for i, j in perm if 0 <= j < count]
    return rider, lax.ppermute(other, axis, perm), odd


def halo(cells, near, far, odd):
    lower = jnp.where(odd, near, far)
    upper = jnp.where(odd, far, near)[:, :HIGH]
    return jnp.concatenate([lower, cells, upper], axis=1)


def cos_sin(phase, period):
    angle = phase.astype(jnp.float32) * (2.0 * math.pi / period)
    return jnp.cos(angle), jnp.sin(angle)


def make_forward(length, after):
    half = length // 2
    lo_count = 64
    hi_count = length // lo_count
    freqs = jnp.arange(half, dtype=jnp.int32)
    hi = jnp.arange(hi_count, dtype=jnp.int32)
    lo = jnp.arange(lo_count, dtype=jnp.int32)
    hi_c, hi_s = cos_sin(hi[:, None] * freqs[None, :] % hi_count, hi_count)
    lo_c, lo_s = cos_sin(lo[:, None] * freqs[None, :] % length, length)
    hi_c, hi_s, lo_c, lo_s, after = lax.optimization_barrier((hi_c, hi_s, lo_c, lo_s, after))
    cos = hi_c[:, None, :] * lo_c[None, :, :] - hi_s[:, None, :] * lo_s[None, :, :]
    sin = hi_s[:, None, :] * lo_c[None, :, :] + hi_c[:, None, :] * lo_s[None, :, :]
    cos = cos.reshape(length, half).astype(jnp.bfloat16)
    sin = sin.reshape(length, half).astype(jnp.bfloat16)
    return cos, sin, after


def inverse_transform(cross, lags):
    count, length = cross.shape
    half = length // 2
    inner = 32
    outer = half // inner
    period = length // inner
    turns = lags // period
    shift = length - lags // 2
    hi = jnp.arange(outer, dtype=jnp.int32)
    lo = jnp.arange(inner, dtype=jnp.int32)
    cols = jnp.arange(period, dtype=jnp.int32)
    laps = jnp.arange(turns, dtype=jnp.int32)
    e_c, e_s = cos_sin(hi[:, None] * cols[None, :] % period, period)
    first = jnp.concatenate(
        [jnp.concatenate([e_c, e_s], axis=1), jnp.concatenate([-e_s, e_c], axis=1)], axis=0
    )
    parts = jnp.concatenate(
        [cross[:, :half].reshape(count, outer, inner), cross[:, half:].reshape(count, outer, inner)],
        axis=1,
    )
    spun = jnp.einsum("rab,am->rbm", parts, first, precision=lax.Precision.HIGHEST)
    u_re, u_im = spun[..., :period], spun[..., period:]
    t_c, t_s = cos_sin(lo[:, None] * (cols[None, :] + shift) % length, length)
    twisted = jnp.concatenate([u_re * t_c - u_im * t_s, u_re * t_s + u_im * t_c], axis=1)
    f_c, f_s = cos_sin(lo[:, None] * laps[None, :] % inner, inner)
    second = jnp.concatenate([f_c, -f_s], axis=0)
    out = jnp.einsum("rbm,bq->rqm", twisted, second, precision=lax.Precision.HIGHEST)
    return out.reshape(count, lags) * (1.0 / math.sqrt(half))


def whiten(spectra, band):
    lead = spectra.shape[:-1]
    width = spectra.shape[-1] // 2
    parts = spectra.reshape(lead + (2, width // band, band))
    power = jnp.sum(parts * parts, axis=(-3, -1)) / (2.0 * band)
    scale = lax.rsqrt(power + 1e-06)
    return (parts * scale[..., None, :, None]).reshape(spectra.shape)


def cross_sum(receivers, emitters):
    half = receivers.shape[-1] // 2
    rec = receivers.astype(jnp.float32)[:, None, None]
    emi = emitters.astype(jnp.float32)[:, :, :, None]
    rec_re, rec_im = (rec[..., :half], rec[..., half:])
    emi_re, emi_im = (emi[..., :half], emi[..., half:])
    real_part = jnp.sum(rec_re * emi_re, axis=0) + jnp.sum(rec_im * emi_im, axis=0)
    imag_part = jnp.sum(rec_im * emi_re, axis=0) - jnp.sum(rec_re * emi_im, axis=0)
    return jnp.concatenate([real_part, imag_part], axis=-1)


def shards(data, sources, owners):
    seg_dev, ch_dev, length = data.shape
    steps, nsrc = sources.shape
    seg_count = lax.axis_size("seg")
    per = ch_dev // seg_count
    here = lax.axis_index("fibre")
    channels = jnp.arange(ch_dev, dtype=jnp.int32)
    keep = (sources[:, :, None] == channels[None, None, :]) & (here == owners)[:, None, None]
    picked = jnp.sum(
        jnp.where(keep.reshape(1, steps * nsrc, ch_dev, 1), data[:, None], jnp.zeros_like(data[:, None])),
        axis=2,
    )
    rider, far, odd = edges(data, "fibre")
    received, near = broadcast(picked, "fibre", rider)
    cos, sin, received = make_forward(length, received)
    window = halo(data, near, far, odd)
    rows = window.shape[1]
    block = jnp.concatenate([window, received], axis=1)
    block = gather(block, "seg")
    segs = block.shape[0]
    flat_rows = block.reshape(segs * block.shape[1], length)
    spectra = jnp.concatenate(
        [
            jnp.dot(flat_rows, cos, preferred_element_type=jnp.float32),
            -jnp.dot(flat_rows, sin, preferred_element_type=jnp.float32),
        ],
        axis=-1,
    )
    white = whiten(spectra.reshape(block.shape), BAND).astype(jnp.bfloat16)
    chosen = white[:, rows:].reshape(segs, steps, nsrc, length)
    start = lax.axis_index("seg") * per
    part = lax.dynamic_slice_in_dim(white[:, :rows], start, per + LOW + HIGH, axis=1)
    total = part[:, 0:per].astype(jnp.float32)
    for offset in range(1, LOW + HIGH + 1):
        total = total + part[:, offset : offset + per].astype(jnp.float32)
    stacked = (total * 0.125).astype(jnp.bfloat16)
    cross = cross_sum(stacked, chosen)
    flat = inverse_transform(cross.reshape(-1, length), LAGS)
    return flat.reshape(steps, nsrc, per, LAGS)


def solution(mesh):
    return jax.shard_map(
        shards,
        mesh=mesh,
        in_specs=(P("seg", "fibre", None), P(), P()),
        out_specs=P(None, None, ("fibre", "seg"), None),
        check_vma=False,
    )
```

```python
import math

import jax
import jax.numpy as jnp
from jax import lax
from jax.sharding import PartitionSpec as P

BAND = 128
LAGS = 1024
LOW = 4
HIGH = 3


def radices(count):
    if count == 64:
        return [2] * 6
    out = []
    while count % 4 == 0:
        out.append(4)
        count //= 4
    while count % 2 == 0:
        out.append(2)
        count //= 2
    if count > 1:
        out.append(count)
    return out


def broadcast(block, axis, rider):
    count = lax.axis_size(axis)
    width = block.shape[1]
    both = lax.ppermute(jnp.concatenate([block, rider], axis=1), axis, [(i, i ^ 1) for i in range(count)])
    block = block + both[:, :width]
    carried = both[:, width:]
    stride = 2
    for radix in radices(count // 2):
        total = block
        for shift in range(1, radix):
            perm = []
            for i in range(count):
                digit = (i // stride) % radix
                perm.append((i, i + ((digit + shift) % radix - digit) * stride))
            total = total + lax.ppermute(block, axis, perm)
        block = total
        stride *= radix
    return block, carried


def gather(block, axis):
    count = lax.axis_size(axis)
    stride = count // 2
    while stride >= 1:
        partner = lax.ppermute(block, axis, [(i, i ^ stride) for i in range(count)])
        block = jnp.concatenate([block, partner], axis=0)
        stride //= 2
    return block


def edges(cells, axis):
    count = lax.axis_size(axis)
    odd = lax.axis_index(axis) % 2 == 1
    rows = cells.shape[1]
    tail = lax.slice_in_dim(cells, rows - LOW, rows, axis=1)
    head = jnp.pad(lax.slice_in_dim(cells, 0, HIGH, axis=1), ((0, 0), (0, LOW - HIGH), (0, 0)))
    rider = jnp.where(odd, head, tail)
    other = jnp.where(odd, tail, head)
    perm = [(i, i + 1) if i % 2 else (i, i - 1) for i in range(count)]
    perm = [(i, j) for i, j in perm if 0 <= j < count]
    return rider, lax.ppermute(other, axis, perm), odd


def halo(cells, near, far, odd):
    lower = jnp.where(odd, near, far)
    upper = jnp.where(odd, far, near)[:, :HIGH]
    return jnp.concatenate([lower, cells, upper], axis=1)


def cos_sin(phase, period):
    angle = phase.astype(jnp.float32) * (2.0 * math.pi / period)
    return jnp.cos(angle), jnp.sin(angle)


def make_forward(length):
    half = length // 2
    lo_count = 64
    hi_count = length // lo_count
    freqs = jnp.arange(half, dtype=jnp.int32)
    hi = jnp.arange(hi_count, dtype=jnp.int32)
    lo = jnp.arange(lo_count, dtype=jnp.int32)
    hi_c, hi_s = cos_sin(hi[:, None] * freqs[None, :] % hi_count, hi_count)
    lo_c, lo_s = cos_sin(lo[:, None] * freqs[None, :] % length, length)
    cos = hi_c[:, None, :] * lo_c[None, :, :] - hi_s[:, None, :] * lo_s[None, :, :]
    sin = hi_s[:, None, :] * lo_c[None, :, :] + hi_c[:, None, :] * lo_s[None, :, :]
    cos = cos.reshape(length, half).astype(jnp.bfloat16)
    sin = sin.reshape(length, half).astype(jnp.bfloat16)
    return cos, sin


def inverse_transform(cross, lags):
    count, length = cross.shape
    half = length // 2
    inner = 32
    outer = half // inner
    period = length // inner
    turns = lags // period
    shift = length - lags // 2
    hi = jnp.arange(outer, dtype=jnp.int32)
    lo = jnp.arange(inner, dtype=jnp.int32)
    cols = jnp.arange(period, dtype=jnp.int32)
    laps = jnp.arange(turns, dtype=jnp.int32)
    e_c, e_s = cos_sin(hi[:, None] * cols[None, :] % period, period)
    first = jnp.concatenate(
        [jnp.concatenate([e_c, e_s], axis=1), jnp.concatenate([-e_s, e_c], axis=1)], axis=0
    )
    parts = jnp.concatenate(
        [cross[:, :half].reshape(count, outer, inner), cross[:, half:].reshape(count, outer, inner)],
        axis=1,
    )
    spun = jnp.einsum("rab,am->rbm", parts, first, precision=lax.Precision.HIGHEST)
    u_re, u_im = spun[..., :period], spun[..., period:]
    t_c, t_s = cos_sin(lo[:, None] * (cols[None, :] + shift) % length, length)
    twisted = jnp.concatenate([u_re * t_c - u_im * t_s, u_re * t_s + u_im * t_c], axis=1)
    f_c, f_s = cos_sin(lo[:, None] * laps[None, :] % inner, inner)
    second = jnp.concatenate([f_c, -f_s], axis=0)
    out = jnp.einsum("rbm,bq->rqm", twisted, second, precision=lax.Precision.HIGHEST)
    return out.reshape(count, lags) * (1.0 / math.sqrt(half))


def whiten(spectra, band):
    lead = spectra.shape[:-1]
    width = spectra.shape[-1] // 2
    parts = spectra.reshape(lead + (2, width // band, band))
    power = jnp.sum(parts * parts, axis=(-3, -1)) / (2.0 * band)
    scale = lax.rsqrt(power + 1e-06)
    return (parts * scale[..., None, :, None]).reshape(spectra.shape)


def cross_sum(receivers, emitters):
    half = receivers.shape[-1] // 2
    rec = receivers.astype(jnp.float32)[:, None, None]
    emi = emitters.astype(jnp.float32)[:, :, :, None]
    rec_re, rec_im = (rec[..., :half], rec[..., half:])
    emi_re, emi_im = (emi[..., :half], emi[..., half:])
    real_part = jnp.sum(rec_re * emi_re, axis=0) + jnp.sum(rec_im * emi_im, axis=0)
    imag_part = jnp.sum(rec_im * emi_re, axis=0) - jnp.sum(rec_re * emi_im, axis=0)
    return jnp.concatenate([real_part, imag_part], axis=-1)


def shards(data, sources, owners):
    seg_dev, ch_dev, length = data.shape
    steps, nsrc = sources.shape
    seg_count = lax.axis_size("seg")
    per = ch_dev // seg_count
    here = lax.axis_index("fibre")
    channels = jnp.arange(ch_dev, dtype=jnp.int32)
    keep = (sources[:, :, None] == channels[None, None, :]) & (here == owners)[:, None, None]
    picked = jnp.sum(
        jnp.where(keep.reshape(1, steps * nsrc, ch_dev, 1), data[:, None], jnp.zeros_like(data[:, None])),
        axis=2,
    )
    rider, far, odd = edges(data, "fibre")
    received, near = broadcast(picked, "fibre", rider)
    window = halo(data, near, far, odd)
    rows = window.shape[1]
    block = jnp.concatenate([window, received], axis=1)
    block = gather(block, "seg")
    segs = block.shape[0]
    cos, sin = make_forward(length)
    flat_rows = block.reshape(segs * block.shape[1], length)
    spectra = jnp.concatenate(
        [
            jnp.dot(flat_rows, cos, preferred_element_type=jnp.float32),
            -jnp.dot(flat_rows, sin, preferred_element_type=jnp.float32),
        ],
        axis=-1,
    )
    white = whiten(spectra.reshape(block.shape), BAND).astype(jnp.bfloat16)
    chosen = white[:, rows:].reshape(segs, steps, nsrc, length)
    start = lax.axis_index("seg") * per
    part = lax.dynamic_slice_in_dim(white[:, :rows], start, per + LOW + HIGH, axis=1)
    total = part[:, 0:per].astype(jnp.float32)
    for offset in range(1, LOW + HIGH + 1):
        total = total + part[:, offset : offset + per].astype(jnp.float32)
    stacked = (total * 0.125).astype(jnp.bfloat16)
    cross = cross_sum(stacked, chosen)
    flat = inverse_transform(cross.reshape(-1, length), LAGS)
    return flat.reshape(steps, nsrc, per, LAGS)


def solution(mesh):
    return jax.shard_map(
        shards,
        mesh=mesh,
        in_specs=(P("seg", "fibre", None), P(), P()),
        out_specs=P(None, None, ("fibre", "seg"), None),
        check_vma=False,
    )
```

```python
import math

import jax
import jax.numpy as jnp
from jax import lax
from jax.sharding import PartitionSpec as P

BAND = 128
LAGS = 1024
LOW = 4
HIGH = 3


def radices(count):
    if count == 64:
        return [2] * 6
    out = []
    while count % 4 == 0:
        out.append(4)
        count //= 4
    while count % 2 == 0:
        out.append(2)
        count //= 2
    if count > 1:
        out.append(count)
    return out


def broadcast(block, axis, rider):
    count = lax.axis_size(axis)
    width = block.shape[1]
    both = lax.ppermute(jnp.concatenate([block, rider], axis=1), axis, [(i, i ^ 1) for i in range(count)])
    block = block + both[:, :width]
    carried = both[:, width:]
    stride = 2
    for radix in radices(count // 2):
        total = block
        for shift in range(1, radix):
            perm = []
            for i in range(count):
                digit = (i // stride) % radix
                perm.append((i, i + ((digit + shift) % radix - digit) * stride))
            total = total + lax.ppermute(block, axis, perm)
        block = total
        stride *= radix
    return block, carried


def gather(block, axis):
    count = lax.axis_size(axis)
    stride = count // 2
    while stride >= 1:
        partner = lax.ppermute(block, axis, [(i, i ^ stride) for i in range(count)])
        block = jnp.concatenate([block, partner], axis=0)
        stride //= 2
    return block


def edges(cells, axis):
    count = lax.axis_size(axis)
    odd = lax.axis_index(axis) % 2 == 1
    rows = cells.shape[1]
    tail = lax.slice_in_dim(cells, rows - LOW, rows, axis=1)
    head = jnp.pad(lax.slice_in_dim(cells, 0, HIGH, axis=1), ((0, 0), (0, LOW - HIGH), (0, 0)))
    rider = jnp.where(odd, head, tail)
    other = jnp.where(odd, tail, head)
    perm = [(i, i + 1) if i % 2 else (i, i - 1) for i in range(count)]
    perm = [(i, j) for i, j in perm if 0 <= j < count]
    return rider, lax.ppermute(other, axis, perm), odd


def halo(cells, near, far, odd):
    lower = jnp.where(odd, near, far)
    upper = jnp.where(odd, far, near)[:, :HIGH]
    return jnp.concatenate([lower, cells, upper], axis=1)


def cos_sin(phase, period):
    angle = phase.astype(jnp.float32) * (2.0 * math.pi / period)
    return jnp.cos(angle), jnp.sin(angle)


def forward_transform(rows):
    count, length = rows.shape
    half = length // 2
    inner = 64
    outer = length // inner
    laps = half // outer
    fine = jnp.arange(inner, dtype=jnp.int32)
    coarse = jnp.arange(outer, dtype=jnp.int32)
    turns = jnp.arange(laps, dtype=jnp.int32)
    w_c, w_s = cos_sin(coarse[:, None] * coarse[None, :] % outer, outer)
    first = jnp.concatenate([w_c, -w_s], axis=1)
    spun = jnp.einsum(
        "rab,ak->rbk",
        rows.reshape(count, outer, inner).astype(jnp.float32),
        first,
        precision=lax.Precision.HIGHEST,
    )
    y_re, y_im = spun[..., :outer], spun[..., outer:]
    t_c, t_s = cos_sin(fine[:, None] * coarse[None, :] % length, length)
    twisted = jnp.concatenate([y_re * t_c + y_im * t_s, y_im * t_c - y_re * t_s], axis=1)
    g_c, g_s = cos_sin(fine[:, None] * turns[None, :] % inner, inner)
    second = jnp.concatenate(
        [jnp.concatenate([g_c, -g_s], axis=1), jnp.concatenate([g_s, g_c], axis=1)], axis=0
    )
    out = jnp.einsum("rnk,nq->rqk", twisted, second, precision=lax.Precision.HIGHEST)
    return jnp.concatenate(
        [out[:, :laps].reshape(count, half), out[:, laps:].reshape(count, half)], axis=-1
    )


def inverse_transform(cross, lags):
    count, length = cross.shape
    half = length // 2
    inner = 32
    outer = half // inner
    period = length // inner
    turns = lags // period
    shift = length - lags // 2
    hi = jnp.arange(outer, dtype=jnp.int32)
    lo = jnp.arange(inner, dtype=jnp.int32)
    cols = jnp.arange(period, dtype=jnp.int32)
    laps = jnp.arange(turns, dtype=jnp.int32)
    e_c, e_s = cos_sin(hi[:, None] * cols[None, :] % period, period)
    first = jnp.concatenate(
        [jnp.concatenate([e_c, e_s], axis=1), jnp.concatenate([-e_s, e_c], axis=1)], axis=0
    )
    parts = jnp.concatenate(
        [cross[:, :half].reshape(count, outer, inner), cross[:, half:].reshape(count, outer, inner)],
        axis=1,
    )
    spun = jnp.einsum("rab,am->rbm", parts, first, precision=lax.Precision.HIGHEST)
    u_re, u_im = spun[..., :period], spun[..., period:]
    t_c, t_s = cos_sin(lo[:, None] * (cols[None, :] + shift) % length, length)
    twisted = jnp.concatenate([u_re * t_c - u_im * t_s, u_re * t_s + u_im * t_c], axis=1)
    f_c, f_s = cos_sin(lo[:, None] * laps[None, :] % inner, inner)
    second = jnp.concatenate([f_c, -f_s], axis=0)
    out = jnp.einsum("rbm,bq->rqm", twisted, second, precision=lax.Precision.HIGHEST)
    return out.reshape(count, lags) * (1.0 / math.sqrt(half))


def whiten(spectra, band):
    lead = spectra.shape[:-1]
    width = spectra.shape[-1] // 2
    parts = spectra.reshape(lead + (2, width // band, band))
    power = jnp.sum(parts * parts, axis=(-3, -1)) / (2.0 * band)
    scale = lax.rsqrt(power + 1e-06)
    return (parts * scale[..., None, :, None]).reshape(spectra.shape)


def cross_sum(receivers, emitters):
    half = receivers.shape[-1] // 2
    rec = receivers.astype(jnp.float32)[:, None, None]
    emi = emitters.astype(jnp.float32)[:, :, :, None]
    rec_re, rec_im = (rec[..., :half], rec[..., half:])
    emi_re, emi_im = (emi[..., :half], emi[..., half:])
    real_part = jnp.sum(rec_re * emi_re, axis=0) + jnp.sum(rec_im * emi_im, axis=0)
    imag_part = jnp.sum(rec_im * emi_re, axis=0) - jnp.sum(rec_re * emi_im, axis=0)
    return jnp.concatenate([real_part, imag_part], axis=-1)


def shards(data, sources, owners):
    seg_dev, ch_dev, length = data.shape
    steps, nsrc = sources.shape
    seg_count = lax.axis_size("seg")
    per = ch_dev // seg_count
    here = lax.axis_index("fibre")
    channels = jnp.arange(ch_dev, dtype=jnp.int32)
    keep = (sources[:, :, None] == channels[None, None, :]) & (here == owners)[:, None, None]
    picked = jnp.sum(
        jnp.where(keep.reshape(1, steps * nsrc, ch_dev, 1), data[:, None], jnp.zeros_like(data[:, None])),
        axis=2,
    )
    rider, far, odd = edges(data, "fibre")
    received, near = broadcast(picked, "fibre", rider)
    window = halo(data, near, far, odd)
    rows = window.shape[1]
    block = jnp.concatenate([window, received], axis=1)
    block = gather(block, "seg")
    segs = block.shape[0]
    spectra = forward_transform(block.reshape(segs * block.shape[1], length))
    white = whiten(spectra.reshape(block.shape), BAND).astype(jnp.bfloat16)
    chosen = white[:, rows:].reshape(segs, steps, nsrc, length)
    start = lax.axis_index("seg") * per
    part = lax.dynamic_slice_in_dim(white[:, :rows], start, per + LOW + HIGH, axis=1)
    total = part[:, 0:per].astype(jnp.float32)
    for offset in range(1, LOW + HIGH + 1):
        total = total + part[:, offset : offset + per].astype(jnp.float32)
    stacked = (total * 0.125).astype(jnp.bfloat16)
    cross = cross_sum(stacked, chosen)
    flat = inverse_transform(cross.reshape(-1, length), LAGS)
    return flat.reshape(steps, nsrc, per, LAGS)


def solution(mesh):
    return jax.shard_map(
        shards,
        mesh=mesh,
        in_specs=(P("seg", "fibre", None), P(), P()),
        out_specs=P(None, None, ("fibre", "seg"), None),
        check_vma=False,
    )
```

```python
import math

import jax
import jax.numpy as jnp
from jax import lax
from jax.sharding import PartitionSpec as P

BAND = 128
LAGS = 1024
LOW = 4
HIGH = 3


def radices(count):
    if count == 64:
        return [2] * 6
    out = []
    while count % 4 == 0:
        out.append(4)
        count //= 4
    while count % 2 == 0:
        out.append(2)
        count //= 2
    if count > 1:
        out.append(count)
    return out


def broadcast(block, axis, rider):
    count = lax.axis_size(axis)
    width = block.shape[1]
    both = lax.ppermute(jnp.concatenate([block, rider], axis=1), axis, [(i, i ^ 1) for i in range(count)])
    block = block + both[:, :width]
    carried = both[:, width:]
    stride = 2
    for radix in radices(count // 2):
        total = block
        for shift in range(1, radix):
            perm = []
            for i in range(count):
                digit = (i // stride) % radix
                perm.append((i, i + ((digit + shift) % radix - digit) * stride))
            total = total + lax.ppermute(block, axis, perm)
        block = total
        stride *= radix
    return block, carried


def gather(block, axis):
    count = lax.axis_size(axis)
    stride = count // 2
    while stride >= 1:
        partner = lax.ppermute(block, axis, [(i, i ^ stride) for i in range(count)])
        block = jnp.concatenate([block, partner], axis=0)
        stride //= 2
    return block


def edges(cells, axis):
    count = lax.axis_size(axis)
    odd = lax.axis_index(axis) % 2 == 1
    rows = cells.shape[1]
    first = jnp.where(odd, 0, rows - LOW)
    rider = lax.dynamic_slice_in_dim(cells, first, LOW, axis=1)
    other = lax.dynamic_slice_in_dim(cells, rows - LOW - first, LOW, axis=1)
    perm = [(i, i + 1) if i % 2 else (i, i - 1) for i in range(count)]
    perm = [(i, j) for i, j in perm if 0 <= j < count]
    return rider, lax.ppermute(other, axis, perm), odd


def halo(cells, near, far, odd):
    lower = jnp.where(odd, near, far)
    upper = jnp.where(odd, far, near)[:, :HIGH]
    return jnp.concatenate([lower, cells, upper], axis=1)


def cos_sin(phase, period):
    angle = phase.astype(jnp.float32) * (2.0 * math.pi / period)
    return jnp.cos(angle), jnp.sin(angle)


def make_forward(length):
    half = length // 2
    lo_count = 64
    hi_count = length // lo_count
    freqs = jnp.arange(half, dtype=jnp.int32)
    hi = jnp.arange(hi_count, dtype=jnp.int32)
    lo = jnp.arange(lo_count, dtype=jnp.int32)
    hi_c, hi_s = cos_sin(hi[:, None] * freqs[None, :] % hi_count, hi_count)
    lo_c, lo_s = cos_sin(lo[:, None] * freqs[None, :] % length, length)
    cos = hi_c[:, None, :] * lo_c[None, :, :] - hi_s[:, None, :] * lo_s[None, :, :]
    sin = hi_s[:, None, :] * lo_c[None, :, :] + hi_c[:, None, :] * lo_s[None, :, :]
    cos = cos.reshape(length, half).astype(jnp.bfloat16)
    sin = sin.reshape(length, half).astype(jnp.bfloat16)
    return cos, sin


def inverse_transform(cross, lags):
    count, length = cross.shape
    half = length // 2
    inner = 32
    outer = half // inner
    period = length // inner
    turns = lags // period
    shift = length - lags // 2
    hi = jnp.arange(outer, dtype=jnp.int32)
    lo = jnp.arange(inner, dtype=jnp.int32)
    cols = jnp.arange(period, dtype=jnp.int32)
    laps = jnp.arange(turns, dtype=jnp.int32)
    e_c, e_s = cos_sin(hi[:, None] * cols[None, :] % period, period)
    first = jnp.concatenate(
        [jnp.concatenate([e_c, e_s], axis=1), jnp.concatenate([-e_s, e_c], axis=1)], axis=0
    )
    parts = jnp.concatenate(
        [cross[:, :half].reshape(count, outer, inner), cross[:, half:].reshape(count, outer, inner)],
        axis=1,
    )
    spun = jnp.einsum("rab,am->rbm", parts, first, precision=lax.Precision.HIGHEST)
    u_re, u_im = spun[..., :period], spun[..., period:]
    t_c, t_s = cos_sin(lo[:, None] * (cols[None, :] + shift) % length, length)
    twisted = jnp.concatenate([u_re * t_c - u_im * t_s, u_re * t_s + u_im * t_c], axis=1)
    f_c, f_s = cos_sin(lo[:, None] * laps[None, :] % inner, inner)
    second = jnp.concatenate([f_c, -f_s], axis=0)
    out = jnp.einsum("rbm,bq->rqm", twisted, second, precision=lax.Precision.HIGHEST)
    return out.reshape(count, lags) * (1.0 / math.sqrt(half))


def whiten(spectra, band):
    lead = spectra.shape[:-1]
    width = spectra.shape[-1] // 2
    parts = spectra.reshape(lead + (2, width // band, band))
    power = jnp.sum(parts * parts, axis=(-3, -1)) / (2.0 * band)
    scale = lax.rsqrt(power + 1e-06)
    return (parts * scale[..., None, :, None]).reshape(spectra.shape)


def cross_sum(receivers, emitters):
    half = receivers.shape[-1] // 2
    rec = receivers.astype(jnp.float32)[:, None, None]
    emi = emitters.astype(jnp.float32)[:, :, :, None]
    rec_re, rec_im = (rec[..., :half], rec[..., half:])
    emi_re, emi_im = (emi[..., :half], emi[..., half:])
    real_part = jnp.sum(rec_re * emi_re, axis=0) + jnp.sum(rec_im * emi_im, axis=0)
    imag_part = jnp.sum(rec_im * emi_re, axis=0) - jnp.sum(rec_re * emi_im, axis=0)
    return jnp.concatenate([real_part, imag_part], axis=-1)


def shards(data, sources, owners):
    seg_dev, ch_dev, length = data.shape
    steps, nsrc = sources.shape
    seg_count = lax.axis_size("seg")
    per = ch_dev // seg_count
    here = lax.axis_index("fibre")
    rows_of = [
        lax.dynamic_slice_in_dim(data, sources[step, j], 1, axis=1)
        for step in range(steps)
        for j in range(nsrc)
    ]
    owned = jnp.repeat(here == owners, nsrc)
    picked = jnp.where(owned[None, :, None], jnp.concatenate(rows_of, axis=1), jnp.zeros_like(data))
    rider, far, odd = edges(data, "fibre")
    received, near = broadcast(picked, "fibre", rider)
    window = halo(data, near, far, odd)
    rows = window.shape[1]
    block = jnp.concatenate([window, received], axis=1)
    block = gather(block, "seg")
    segs = block.shape[0]
    cos, sin = make_forward(length)
    flat_rows = block.reshape(segs * block.shape[1], length)
    spectra = jnp.concatenate(
        [
            jnp.dot(flat_rows, cos, preferred_element_type=jnp.float32),
            -jnp.dot(flat_rows, sin, preferred_element_type=jnp.float32),
        ],
        axis=-1,
    )
    white = whiten(spectra.reshape(block.shape), BAND).astype(jnp.bfloat16)
    chosen = white[:, rows:].reshape(segs, steps, nsrc, length)
    start = lax.axis_index("seg") * per
    part = lax.dynamic_slice_in_dim(white[:, :rows], start, per + LOW + HIGH, axis=1)
    total = part[:, 0:per].astype(jnp.float32)
    for offset in range(1, LOW + HIGH + 1):
        total = total + part[:, offset : offset + per].astype(jnp.float32)
    stacked = (total * 0.125).astype(jnp.bfloat16)
    cross = cross_sum(stacked, chosen)
    flat = inverse_transform(cross.reshape(-1, length), LAGS)
    return flat.reshape(steps, nsrc, per, LAGS)


def solution(mesh):
    return jax.shard_map(
        shards,
        mesh=mesh,
        in_specs=(P("seg", "fibre", None), P(), P()),
        out_specs=P(None, None, ("fibre", "seg"), None),
        check_vma=False,
    )
```

```python
import math

import jax
import jax.numpy as jnp
from jax import lax
from jax.sharding import PartitionSpec as P

BAND = 128
LAGS = 1024
LOW = 4
HIGH = 3


def broadcast(block, axis, rider):
    count = lax.axis_size(axis)
    width = block.shape[1]
    both = lax.ppermute(jnp.concatenate([block, rider], axis=1), axis, [(i, i ^ 1) for i in range(count)])
    block = block + both[:, :width]
    carried = both[:, width:]
    strides = [1 << bit for bit in range(1, count.bit_length() - 1)]
    if count == 128:
        strides = [8, 4, 2, 16, 32, 64]
    for stride in strides:
        block = block + lax.ppermute(block, axis, [(i, i ^ stride) for i in range(count)])
    return block, carried


def gather(block, axis):
    count = lax.axis_size(axis)
    stride = count // 2
    while stride >= 1:
        partner = lax.ppermute(block, axis, [(i, i ^ stride) for i in range(count)])
        block = jnp.concatenate([block, partner], axis=0)
        stride //= 2
    return block


def edges(cells, axis):
    count = lax.axis_size(axis)
    odd = lax.axis_index(axis) % 2 == 1
    rows = cells.shape[1]
    tail = lax.slice_in_dim(cells, rows - LOW, rows, axis=1)
    head = jnp.pad(lax.slice_in_dim(cells, 0, HIGH, axis=1), ((0, 0), (0, LOW - HIGH), (0, 0)))
    rider = jnp.where(odd, head, tail)
    other = jnp.where(odd, tail, head)
    perm = [(i, i + 1) if i % 2 else (i, i - 1) for i in range(count)]
    perm = [(i, j) for i, j in perm if 0 <= j < count]
    return rider, lax.ppermute(other, axis, perm), odd


def halo(cells, near, far, odd):
    lower = jnp.where(odd, near, far)
    upper = jnp.where(odd, far, near)[:, :HIGH]
    return jnp.concatenate([lower, cells, upper], axis=1)


def cos_sin(phase, period):
    angle = phase.astype(jnp.float32) * (2.0 * math.pi / period)
    return jnp.cos(angle), jnp.sin(angle)


def make_forward(length):
    half = length // 2
    lo_count = 64
    hi_count = length // lo_count
    freqs = jnp.arange(half, dtype=jnp.int32)
    hi = jnp.arange(hi_count, dtype=jnp.int32)
    lo = jnp.arange(lo_count, dtype=jnp.int32)
    hi_c, hi_s = cos_sin(hi[:, None] * freqs[None, :] % hi_count, hi_count)
    lo_c, lo_s = cos_sin(lo[:, None] * freqs[None, :] % length, length)
    cos = hi_c[:, None, :] * lo_c[None, :, :] - hi_s[:, None, :] * lo_s[None, :, :]
    sin = hi_s[:, None, :] * lo_c[None, :, :] + hi_c[:, None, :] * lo_s[None, :, :]
    cos = cos.reshape(length, half).astype(jnp.bfloat16)
    sin = sin.reshape(length, half).astype(jnp.bfloat16)
    return cos, sin


def inverse_transform(cross, lags):
    count, length = cross.shape
    half = length // 2
    inner = 32
    outer = half // inner
    period = length // inner
    turns = lags // period
    shift = length - lags // 2
    hi = jnp.arange(outer, dtype=jnp.int32)
    lo = jnp.arange(inner, dtype=jnp.int32)
    cols = jnp.arange(period, dtype=jnp.int32)
    laps = jnp.arange(turns, dtype=jnp.int32)
    e_c, e_s = cos_sin(hi[:, None] * cols[None, :] % period, period)
    first = jnp.concatenate(
        [jnp.concatenate([e_c, e_s], axis=1), jnp.concatenate([-e_s, e_c], axis=1)], axis=0
    )
    parts = jnp.concatenate(
        [cross[:, :half].reshape(count, outer, inner), cross[:, half:].reshape(count, outer, inner)],
        axis=1,
    )
    spun = jnp.einsum("rab,am->rbm", parts, first, precision=lax.Precision.HIGHEST)
    u_re, u_im = spun[..., :period], spun[..., period:]
    t_c, t_s = cos_sin(lo[:, None] * (cols[None, :] + shift) % length, length)
    twisted = jnp.concatenate([u_re * t_c - u_im * t_s, u_re * t_s + u_im * t_c], axis=1)
    f_c, f_s = cos_sin(lo[:, None] * laps[None, :] % inner, inner)
    second = jnp.concatenate([f_c, -f_s], axis=0)
    out = jnp.einsum("rbm,bq->rqm", twisted, second, precision=lax.Precision.HIGHEST)
    return out.reshape(count, lags) * (1.0 / math.sqrt(half))


def whiten(spectra, band):
    lead = spectra.shape[:-1]
    width = spectra.shape[-1] // 2
    parts = spectra.reshape(lead + (2, width // band, band))
    power = jnp.sum(parts * parts, axis=(-3, -1)) / (2.0 * band)
    scale = lax.rsqrt(power + 1e-06)
    return (parts * scale[..., None, :, None]).reshape(spectra.shape)


def cross_sum(receivers, emitters):
    half = receivers.shape[-1] // 2
    rec = receivers.astype(jnp.float32)[:, None, None]
    emi = emitters.astype(jnp.float32)[:, :, :, None]
    rec_re, rec_im = (rec[..., :half], rec[..., half:])
    emi_re, emi_im = (emi[..., :half], emi[..., half:])
    real_part = jnp.sum(rec_re * emi_re, axis=0) + jnp.sum(rec_im * emi_im, axis=0)
    imag_part = jnp.sum(rec_im * emi_re, axis=0) - jnp.sum(rec_re * emi_im, axis=0)
    return jnp.concatenate([real_part, imag_part], axis=-1)


def shards(data, sources, owners):
    seg_dev, ch_dev, length = data.shape
    steps, nsrc = sources.shape
    seg_count = lax.axis_size("seg")
    per = ch_dev // seg_count
    here = lax.axis_index("fibre")
    channels = jnp.arange(ch_dev, dtype=jnp.int32)
    keep = (sources[:, :, None] == channels[None, None, :]) & (here == owners)[:, None, None]
    picked = jnp.sum(
        jnp.where(keep.reshape(1, steps * nsrc, ch_dev, 1), data[:, None], jnp.zeros_like(data[:, None])),
        axis=2,
    )
    rider, far, odd = edges(data, "fibre")
    received, near = broadcast(picked, "fibre", rider)
    window = halo(data, near, far, odd)
    rows = window.shape[1]
    block = jnp.concatenate([window, received], axis=1)
    block = gather(block, "seg")
    segs = block.shape[0]
    cos, sin = make_forward(length)
    flat_rows = block.reshape(segs * block.shape[1], length)
    spectra = jnp.concatenate(
        [
            jnp.dot(flat_rows, cos, preferred_element_type=jnp.float32),
            -jnp.dot(flat_rows, sin, preferred_element_type=jnp.float32),
        ],
        axis=-1,
    )
    white = whiten(spectra.reshape(block.shape), BAND).astype(jnp.bfloat16)
    chosen = white[:, rows:].reshape(segs, steps, nsrc, length)
    start = lax.axis_index("seg") * per
    part = lax.dynamic_slice_in_dim(white[:, :rows], start, per + LOW + HIGH, axis=1)
    total = part[:, 0:per].astype(jnp.float32)
    for offset in range(1, LOW + HIGH + 1):
        total = total + part[:, offset : offset + per].astype(jnp.float32)
    stacked = (total * 0.125).astype(jnp.bfloat16)
    cross = cross_sum(stacked, chosen)
    flat = inverse_transform(cross.reshape(-1, length), LAGS)
    return flat.reshape(steps, nsrc, per, LAGS)


def solution(mesh):
    return jax.shard_map(
        shards,
        mesh=mesh,
        in_specs=(P("seg", "fibre", None), P(), P()),
        out_specs=P(None, None, ("fibre", "seg"), None),
        check_vma=False,
    )
```

```python
import math

import jax
import jax.numpy as jnp
from jax import lax
from jax.sharding import PartitionSpec as P

BAND = 128
LAGS = 1024
LOW = 4
HIGH = 3


def broadcast(block, axis, rider):
    count = lax.axis_size(axis)
    width = block.shape[1]
    both = lax.ppermute(jnp.concatenate([block, rider], axis=1), axis, [(i, i ^ 1) for i in range(count)])
    block = block + both[:, :width]
    carried = both[:, width:]
    strides = [1 << bit for bit in range(1, count.bit_length() - 1)]
    if count == 128:
        strides = [8, 4, 2, 16, 32, 64]
    for stride in strides:
        block = block + lax.ppermute(block, axis, [(i, i ^ stride) for i in range(count)])
    return block, carried


def gather(block, axis):
    count = lax.axis_size(axis)
    stride = count // 2
    while stride >= 1:
        partner = lax.ppermute(block, axis, [(i, i ^ stride) for i in range(count)])
        block = jnp.concatenate([block, partner], axis=0)
        stride //= 2
    return block


def edges(cells, axis):
    count = lax.axis_size(axis)
    odd = lax.axis_index(axis) % 2 == 1
    rows = cells.shape[1]
    tail = lax.slice_in_dim(cells, rows - LOW, rows, axis=1)
    head = jnp.pad(lax.slice_in_dim(cells, 0, HIGH, axis=1), ((0, 0), (0, LOW - HIGH), (0, 0)))
    rider = jnp.where(odd, head, tail)
    other = jnp.where(odd, tail, head)
    perm = [(i, i + 1) if i % 2 else (i, i - 1) for i in range(count)]
    perm = [(i, j) for i, j in perm if 0 <= j < count]
    return rider, lax.ppermute(other, axis, perm), odd


def halo(cells, near, far, odd):
    lower = jnp.where(odd, near, far)
    upper = jnp.where(odd, far, near)[:, :HIGH]
    return jnp.concatenate([lower, cells, upper], axis=1)


def cos_sin(phase, period):
    angle = phase.astype(jnp.float32) * (2.0 * math.pi / period)
    return jnp.cos(angle), jnp.sin(angle)


def make_forward(length):
    half = length // 2
    lo_count = 64
    period = length // lo_count
    freqs = jnp.arange(half, dtype=jnp.int32)
    hi = jnp.arange(half // lo_count, dtype=jnp.int32)
    lo = jnp.arange(lo_count, dtype=jnp.int32)
    hi_c, hi_s = cos_sin(hi[:, None] * freqs[None, :] % period, period)
    lo_c, lo_s = cos_sin(lo[:, None] * freqs[None, :] % length, length)
    cos = hi_c[:, None, :] * lo_c[None, :, :] - hi_s[:, None, :] * lo_s[None, :, :]
    sin = hi_s[:, None, :] * lo_c[None, :, :] + hi_c[:, None, :] * lo_s[None, :, :]
    cos = cos.reshape(half, half).astype(jnp.bfloat16)
    sin = sin.reshape(half, half).astype(jnp.bfloat16)
    return cos, sin


def split(values):
    high = values.astype(jnp.bfloat16)
    low = (values - high.astype(jnp.float32)).astype(jnp.bfloat16)
    return jnp.concatenate([high, low], axis=0)


def forward_transform(rows, cos, sin):
    count, length = rows.shape
    half = length // 2
    wide = rows.astype(jnp.float32)
    front = wide[:, :half]
    mirror = jnp.concatenate([wide[:, :1], wide[:, : half : -1]], axis=1)
    first = (jnp.arange(half) == 0)[None, :]
    even = front + jnp.where(first, 0.0, mirror)
    odd = front - jnp.where(first, front, mirror)
    sign = 1.0 - 2.0 * (jnp.arange(half) % 2).astype(jnp.float32)
    real = jnp.dot(split(even), cos, preferred_element_type=jnp.float32)
    imag = jnp.dot(split(odd), sin, preferred_element_type=jnp.float32)
    real = real[:count] + real[count:] + wide[:, half : half + 1] * sign[None, :]
    imag = -(imag[:count] + imag[count:])
    return jnp.concatenate([real, imag], axis=-1)


def inverse_transform(cross, lags):
    count, length = cross.shape
    half = length // 2
    inner = 32
    outer = half // inner
    period = length // inner
    turns = lags // period
    shift = length - lags // 2
    hi = jnp.arange(outer, dtype=jnp.int32)
    lo = jnp.arange(inner, dtype=jnp.int32)
    cols = jnp.arange(period, dtype=jnp.int32)
    laps = jnp.arange(turns, dtype=jnp.int32)
    e_c, e_s = cos_sin(hi[:, None] * cols[None, :] % period, period)
    first = jnp.concatenate(
        [jnp.concatenate([e_c, e_s], axis=1), jnp.concatenate([-e_s, e_c], axis=1)], axis=0
    )
    parts = jnp.concatenate(
        [cross[:, :half].reshape(count, outer, inner), cross[:, half:].reshape(count, outer, inner)],
        axis=1,
    )
    spun = jnp.einsum("rab,am->rbm", parts, first, precision=lax.Precision.HIGHEST)
    u_re, u_im = spun[..., :period], spun[..., period:]
    t_c, t_s = cos_sin(lo[:, None] * (cols[None, :] + shift) % length, length)
    twisted = jnp.concatenate([u_re * t_c - u_im * t_s, u_re * t_s + u_im * t_c], axis=1)
    f_c, f_s = cos_sin(lo[:, None] * laps[None, :] % inner, inner)
    second = jnp.concatenate([f_c, -f_s], axis=0)
    out = jnp.einsum("rbm,bq->rqm", twisted, second, precision=lax.Precision.HIGHEST)
    return out.reshape(count, lags) * (1.0 / math.sqrt(half))


def whiten(spectra, band):
    lead = spectra.shape[:-1]
    width = spectra.shape[-1] // 2
    parts = spectra.reshape(lead + (2, width // band, band))
    power = jnp.sum(parts * parts, axis=(-3, -1)) / (2.0 * band)
    scale = lax.rsqrt(power + 1e-06)
    return (parts * scale[..., None, :, None]).reshape(spectra.shape)


def cross_sum(receivers, emitters):
    half = receivers.shape[-1] // 2
    rec = receivers.astype(jnp.float32)[:, None, None]
    emi = emitters.astype(jnp.float32)[:, :, :, None]
    rec_re, rec_im = (rec[..., :half], rec[..., half:])
    emi_re, emi_im = (emi[..., :half], emi[..., half:])
    real_part = jnp.sum(rec_re * emi_re, axis=0) + jnp.sum(rec_im * emi_im, axis=0)
    imag_part = jnp.sum(rec_im * emi_re, axis=0) - jnp.sum(rec_re * emi_im, axis=0)
    return jnp.concatenate([real_part, imag_part], axis=-1)


def shards(data, sources, owners):
    seg_dev, ch_dev, length = data.shape
    steps, nsrc = sources.shape
    seg_count = lax.axis_size("seg")
    per = ch_dev // seg_count
    here = lax.axis_index("fibre")
    channels = jnp.arange(ch_dev, dtype=jnp.int32)
    keep = (sources[:, :, None] == channels[None, None, :]) & (here == owners)[:, None, None]
    picked = jnp.sum(
        jnp.where(keep.reshape(1, steps * nsrc, ch_dev, 1), data[:, None], jnp.zeros_like(data[:, None])),
        axis=2,
    )
    rider, far, odd = edges(data, "fibre")
    received, near = broadcast(picked, "fibre", rider)
    window = halo(data, near, far, odd)
    rows = window.shape[1]
    block = jnp.concatenate([window, received], axis=1)
    block = gather(block, "seg")
    segs = block.shape[0]
    cos, sin = make_forward(length)
    spectra = forward_transform(block.reshape(segs * block.shape[1], length), cos, sin)
    white = whiten(spectra.reshape(block.shape), BAND).astype(jnp.bfloat16)
    chosen = white[:, rows:].reshape(segs, steps, nsrc, length)
    start = lax.axis_index("seg") * per
    part = lax.dynamic_slice_in_dim(white[:, :rows], start, per + LOW + HIGH, axis=1)
    total = part[:, 0:per].astype(jnp.float32)
    for offset in range(1, LOW + HIGH + 1):
        total = total + part[:, offset : offset + per].astype(jnp.float32)
    stacked = (total * 0.125).astype(jnp.bfloat16)
    cross = cross_sum(stacked, chosen)
    flat = inverse_transform(cross.reshape(-1, length), LAGS)
    return flat.reshape(steps, nsrc, per, LAGS)


def solution(mesh):
    return jax.shard_map(
        shards,
        mesh=mesh,
        in_specs=(P("seg", "fibre", None), P(), P()),
        out_specs=P(None, None, ("fibre", "seg"), None),
        check_vma=False,
    )
```

```python
import math

import jax
import jax.numpy as jnp
from jax import lax
from jax.sharding import PartitionSpec as P

BAND = 128
LAGS = 1024
LOW = 4
HIGH = 3


def broadcast(block, axis, rider):
    count = lax.axis_size(axis)
    width = block.shape[1]
    both = lax.ppermute(jnp.concatenate([block, rider], axis=1), axis, [(i, i ^ 1) for i in range(count)])
    block = block + both[:, :width]
    carried = both[:, width:]
    strides = [1 << bit for bit in range(1, count.bit_length() - 1)]
    if count == 128:
        strides = [8, 4, 2, 16, 32, 64]
    for stride in strides:
        block = block + lax.ppermute(block, axis, [(i, i ^ stride) for i in range(count)])
    return block, carried


def gather(block, axis):
    count = lax.axis_size(axis)
    stride = count // 2
    while stride >= 1:
        partner = lax.ppermute(block, axis, [(i, i ^ stride) for i in range(count)])
        block = jnp.concatenate([block, partner], axis=0)
        stride //= 2
    return block


def edges(cells, axis):
    count = lax.axis_size(axis)
    odd = lax.axis_index(axis) % 2 == 1
    rows = cells.shape[1]
    tail = lax.slice_in_dim(cells, rows - LOW, rows, axis=1)
    head = jnp.pad(lax.slice_in_dim(cells, 0, HIGH, axis=1), ((0, 0), (0, LOW - HIGH), (0, 0)))
    rider = jnp.where(odd, head, tail)
    other = jnp.where(odd, tail, head)
    perm = [(i, i + 1) if i % 2 else (i, i - 1) for i in range(count)]
    perm = [(i, j) for i, j in perm if 0 <= j < count]
    return rider, lax.ppermute(other, axis, perm), odd


def halo(cells, near, far, odd):
    lower = jnp.where(odd, near, far)
    upper = jnp.where(odd, far, near)[:, :HIGH]
    return jnp.concatenate([lower, cells, upper], axis=1)


def cos_sin(phase, period):
    angle = phase.astype(jnp.float32) * (2.0 * math.pi / period)
    return jnp.cos(angle), jnp.sin(angle)


def make_forward(length):
    half = length // 2
    lo_count = 64
    hi_count = length // lo_count
    freqs = jnp.arange(half, dtype=jnp.int32)
    hi = jnp.arange(hi_count, dtype=jnp.int32)
    lo = jnp.arange(lo_count, dtype=jnp.int32)
    hi_c, hi_s = cos_sin(hi[:, None] * freqs[None, :] % hi_count, hi_count)
    lo_c, lo_s = cos_sin(lo[:, None] * freqs[None, :] % length, length)
    cos = hi_c[:, None, :] * lo_c[None, :, :] - hi_s[:, None, :] * lo_s[None, :, :]
    sin = hi_s[:, None, :] * lo_c[None, :, :] + hi_c[:, None, :] * lo_s[None, :, :]
    cos = cos.reshape(length, half).astype(jnp.bfloat16)
    sin = sin.reshape(length, half).astype(jnp.bfloat16)
    return cos, sin


def chunked_forward(rows, length, pieces):
    half = length // 2
    lo_count = 64
    hi_count = length // lo_count
    step = hi_count // pieces
    freqs = jnp.arange(half, dtype=jnp.int32)
    lo = jnp.arange(lo_count, dtype=jnp.int32)
    lo_c, lo_s = cos_sin(lo[:, None] * freqs[None, :] % length, length)
    real = None
    imag = None
    for piece in range(pieces):
        hi = jnp.arange(piece * step, (piece + 1) * step, dtype=jnp.int32)
        hi_c, hi_s = cos_sin(hi[:, None] * freqs[None, :] % hi_count, hi_count)
        cos = hi_c[:, None, :] * lo_c[None, :, :] - hi_s[:, None, :] * lo_s[None, :, :]
        sin = hi_s[:, None, :] * lo_c[None, :, :] + hi_c[:, None, :] * lo_s[None, :, :]
        cos = cos.reshape(step * lo_count, half).astype(jnp.bfloat16)
        sin = sin.reshape(step * lo_count, half).astype(jnp.bfloat16)
        part = rows[:, piece * step * lo_count : (piece + 1) * step * lo_count]
        re = jnp.dot(part, cos, preferred_element_type=jnp.float32)
        im = jnp.dot(part, sin, preferred_element_type=jnp.float32)
        real = re if real is None else real + re
        imag = im if imag is None else imag + im
    return jnp.concatenate([real, -imag], axis=-1)


def inverse_transform(cross, lags):
    count, length = cross.shape
    half = length // 2
    inner = 32
    outer = half // inner
    period = length // inner
    turns = lags // period
    shift = length - lags // 2
    hi = jnp.arange(outer, dtype=jnp.int32)
    lo = jnp.arange(inner, dtype=jnp.int32)
    cols = jnp.arange(period, dtype=jnp.int32)
    laps = jnp.arange(turns, dtype=jnp.int32)
    e_c, e_s = cos_sin(hi[:, None] * cols[None, :] % period, period)
    first = jnp.concatenate(
        [jnp.concatenate([e_c, e_s], axis=1), jnp.concatenate([-e_s, e_c], axis=1)], axis=0
    )
    parts = jnp.concatenate(
        [cross[:, :half].reshape(count, outer, inner), cross[:, half:].reshape(count, outer, inner)],
        axis=1,
    )
    spun = jnp.einsum("rab,am->rbm", parts, first, precision=lax.Precision.HIGHEST)
    u_re, u_im = spun[..., :period], spun[..., period:]
    t_c, t_s = cos_sin(lo[:, None] * (cols[None, :] + shift) % length, length)
    twisted = jnp.concatenate([u_re * t_c - u_im * t_s, u_re * t_s + u_im * t_c], axis=1)
    f_c, f_s = cos_sin(lo[:, None] * laps[None, :] % inner, inner)
    second = jnp.concatenate([f_c, -f_s], axis=0)
    out = jnp.einsum("rbm,bq->rqm", twisted, second, precision=lax.Precision.HIGHEST)
    return out.reshape(count, lags) * (1.0 / math.sqrt(half))


def whiten(spectra, band):
    lead = spectra.shape[:-1]
    width = spectra.shape[-1] // 2
    parts = spectra.reshape(lead + (2, width // band, band))
    power = jnp.sum(parts * parts, axis=(-3, -1)) / (2.0 * band)
    scale = lax.rsqrt(power + 1e-06)
    return (parts * scale[..., None, :, None]).reshape(spectra.shape)


def cross_sum(receivers, emitters):
    half = receivers.shape[-1] // 2
    rec = receivers.astype(jnp.float32)[:, None, None]
    emi = emitters.astype(jnp.float32)[:, :, :, None]
    rec_re, rec_im = (rec[..., :half], rec[..., half:])
    emi_re, emi_im = (emi[..., :half], emi[..., half:])
    real_part = jnp.sum(rec_re * emi_re, axis=0) + jnp.sum(rec_im * emi_im, axis=0)
    imag_part = jnp.sum(rec_im * emi_re, axis=0) - jnp.sum(rec_re * emi_im, axis=0)
    return jnp.concatenate([real_part, imag_part], axis=-1)


def shards(data, sources, owners):
    seg_dev, ch_dev, length = data.shape
    steps, nsrc = sources.shape
    seg_count = lax.axis_size("seg")
    per = ch_dev // seg_count
    here = lax.axis_index("fibre")
    channels = jnp.arange(ch_dev, dtype=jnp.int32)
    keep = (sources[:, :, None] == channels[None, None, :]) & (here == owners)[:, None, None]
    picked = jnp.sum(
        jnp.where(keep.reshape(1, steps * nsrc, ch_dev, 1), data[:, None], jnp.zeros_like(data[:, None])),
        axis=2,
    )
    rider, far, odd = edges(data, "fibre")
    received, near = broadcast(picked, "fibre", rider)
    window = halo(data, near, far, odd)
    rows = window.shape[1]
    block = jnp.concatenate([window, received], axis=1)
    block = gather(block, "seg")
    segs = block.shape[0]
    spectra = chunked_forward(block.reshape(segs * block.shape[1], length), length, 4)
    white = whiten(spectra.reshape(block.shape), BAND).astype(jnp.bfloat16)
    chosen = white[:, rows:].reshape(segs, steps, nsrc, length)
    start = lax.axis_index("seg") * per
    part = lax.dynamic_slice_in_dim(white[:, :rows], start, per + LOW + HIGH, axis=1)
    total = part[:, 0:per].astype(jnp.float32)
    for offset in range(1, LOW + HIGH + 1):
        total = total + part[:, offset : offset + per].astype(jnp.float32)
    stacked = (total * 0.125).astype(jnp.bfloat16)
    cross = cross_sum(stacked, chosen)
    flat = inverse_transform(cross.reshape(-1, length), LAGS)
    return flat.reshape(steps, nsrc, per, LAGS)


def solution(mesh):
    return jax.shard_map(
        shards,
        mesh=mesh,
        in_specs=(P("seg", "fibre", None), P(), P()),
        out_specs=P(None, None, ("fibre", "seg"), None),
        check_vma=False,
    )
```

```python
import math

import jax
import jax.numpy as jnp
from jax import lax
from jax.sharding import PartitionSpec as P

BAND = 128
LAGS = 1024
LOW = 4
HIGH = 3


def broadcast(block, axis, rider):
    count = lax.axis_size(axis)
    width = block.shape[1]
    both = lax.ppermute(jnp.concatenate([block, rider], axis=1), axis, [(i, i ^ 1) for i in range(count)])
    block = block + both[:, :width]
    carried = both[:, width:]
    strides = [1 << bit for bit in range(1, count.bit_length() - 1)]
    if count == 128:
        strides = [8, 4, 2, 16, 32, 64]
    for stride in strides:
        block = block + lax.ppermute(block, axis, [(i, i ^ stride) for i in range(count)])
    return block, carried


def gather(block, axis):
    count = lax.axis_size(axis)
    stride = count // 2
    while stride >= 1:
        partner = lax.ppermute(block, axis, [(i, i ^ stride) for i in range(count)])
        block = jnp.concatenate([block, partner], axis=0)
        stride //= 2
    return block


def edges(cells, axis):
    count = lax.axis_size(axis)
    odd = lax.axis_index(axis) % 2 == 1
    rows = cells.shape[1]
    tail = lax.slice_in_dim(cells, rows - LOW, rows, axis=1)
    head = jnp.pad(lax.slice_in_dim(cells, 0, HIGH, axis=1), ((0, 0), (0, LOW - HIGH), (0, 0)))
    rider = jnp.where(odd, head, tail)
    other = jnp.where(odd, tail, head)
    perm = [(i, i + 1) if i % 2 else (i, i - 1) for i in range(count)]
    perm = [(i, j) for i, j in perm if 0 <= j < count]
    return rider, lax.ppermute(other, axis, perm), odd


def halo(cells, near, far, odd):
    lower = jnp.where(odd, near, far)
    upper = jnp.where(odd, far, near)[:, :HIGH]
    return jnp.concatenate([lower, cells, upper], axis=1)


def cos_sin(phase, period):
    angle = phase.astype(jnp.float32) * (2.0 * math.pi / period)
    return jnp.cos(angle), jnp.sin(angle)


def make_forward(length):
    half = length // 2
    lo_count = 64
    hi_count = length // lo_count
    freqs = jnp.arange(half, dtype=jnp.int32)
    hi = jnp.arange(hi_count, dtype=jnp.int32)
    lo = jnp.arange(lo_count, dtype=jnp.int32)
    hi_c, hi_s = cos_sin(hi[:, None] * freqs[None, :] % hi_count, hi_count)
    lo_c, lo_s = cos_sin(lo[:, None] * freqs[None, :] % length, length)
    cos = hi_c[:, None, :] * lo_c[None, :, :] - hi_s[:, None, :] * lo_s[None, :, :]
    sin = hi_s[:, None, :] * lo_c[None, :, :] + hi_c[:, None, :] * lo_s[None, :, :]
    cos = cos.reshape(length, half).astype(jnp.bfloat16)
    sin = sin.reshape(length, half).astype(jnp.bfloat16)
    return cos, sin


def inverse_transform(cross, lags):
    count, length = cross.shape
    half = length // 2
    inner = 32
    outer = half // inner
    period = length // inner
    turns = lags // period
    shift = length - lags // 2
    hi = jnp.arange(outer, dtype=jnp.int32)
    lo = jnp.arange(inner, dtype=jnp.int32)
    cols = jnp.arange(period, dtype=jnp.int32)
    laps = jnp.arange(turns, dtype=jnp.int32)
    e_c, e_s = cos_sin(hi[:, None] * cols[None, :] % period, period)
    first = jnp.concatenate(
        [jnp.concatenate([e_c, e_s], axis=1), jnp.concatenate([-e_s, e_c], axis=1)], axis=0
    )
    parts = jnp.concatenate(
        [cross[:, :half].reshape(count, outer, inner), cross[:, half:].reshape(count, outer, inner)],
        axis=1,
    )
    spun = jnp.einsum("rab,am->rbm", parts, first, precision=lax.Precision.HIGHEST)
    u_re, u_im = spun[..., :period], spun[..., period:]
    t_c, t_s = cos_sin(lo[:, None] * (cols[None, :] + shift) % length, length)
    twisted = jnp.concatenate([u_re * t_c - u_im * t_s, u_re * t_s + u_im * t_c], axis=1)
    f_c, f_s = cos_sin(lo[:, None] * laps[None, :] % inner, inner)
    second = jnp.concatenate([f_c, -f_s], axis=0)
    out = jnp.einsum("rbm,bq->rqm", twisted, second, precision=lax.Precision.HIGHEST)
    return out.reshape(count, lags) * (1.0 / math.sqrt(half))


def whiten(spectra, band):
    lead = spectra.shape[:-1]
    width = spectra.shape[-1] // 2
    parts = spectra.reshape(lead + (2, width // band, band))
    power = jnp.sum(parts * parts, axis=(-3, -1)) / (2.0 * band)
    scale = lax.rsqrt(power + 1e-06)
    return (parts * scale[..., None, :, None]).reshape(spectra.shape)


def cross_sum(receivers, emitters):
    half = receivers.shape[-1] // 2
    rec = receivers.astype(jnp.float32)[:, None, None]
    emi = emitters.astype(jnp.float32)[:, :, :, None]
    rec_re, rec_im = (rec[..., :half], rec[..., half:])
    emi_re, emi_im = (emi[..., :half], emi[..., half:])
    real_part = jnp.sum(rec_re * emi_re, axis=0) + jnp.sum(rec_im * emi_im, axis=0)
    imag_part = jnp.sum(rec_im * emi_re, axis=0) - jnp.sum(rec_re * emi_im, axis=0)
    return jnp.concatenate([real_part, imag_part], axis=-1)


def shards(data, sources, owners):
    seg_dev, ch_dev, length = data.shape
    steps, nsrc = sources.shape
    seg_count = lax.axis_size("seg")
    per = ch_dev // seg_count
    here = lax.axis_index("fibre")
    channels = jnp.arange(ch_dev, dtype=jnp.int32)
    keep = (sources[:, :, None] == channels[None, None, :]) & (here == owners)[:, None, None]
    picked = jnp.sum(
        jnp.where(keep.reshape(1, steps * nsrc, ch_dev, 1), data[:, None], jnp.zeros_like(data[:, None])),
        axis=2,
    )
    rider, far, odd = edges(data, "fibre")
    received, near = broadcast(picked, "fibre", rider)
    window = halo(data, near, far, odd)
    rows = per + LOW + HIGH
    mine_at = lax.axis_index("seg")
    if seg_count == 4:
        span = rows + per
        lead = lax.dynamic_slice_in_dim(window, 2 * per * (1 - mine_at // 2), span, axis=1)
        first = lax.ppermute(
            jnp.concatenate([lead, received], axis=1), "seg", [(i, i ^ 2) for i in range(4)]
        )
        far_win, far_src = first[:, :span], first[:, span:]
        pair = jnp.bitwise_xor(mine_at, 1)
        base = 2 * per * (mine_at // 2)
        sent = jnp.concatenate(
            [
                jnp.concatenate(
                    [lax.dynamic_slice_in_dim(window, per * pair, rows, axis=1), received], axis=1
                ),
                jnp.concatenate(
                    [lax.dynamic_slice_in_dim(far_win, per * pair - base, rows, axis=1), far_src],
                    axis=1,
                ),
            ],
            axis=0,
        )
        second = lax.ppermute(sent, "seg", [(i, i ^ 1) for i in range(4)])
        own = jnp.concatenate(
            [lax.dynamic_slice_in_dim(window, per * mine_at, rows, axis=1), received], axis=1
        )
        beside = jnp.concatenate(
            [lax.dynamic_slice_in_dim(far_win, per * mine_at - base, rows, axis=1), far_src], axis=1
        )
        block = jnp.concatenate([own, beside, second], axis=0)
    else:
        block = gather(jnp.concatenate([window, received], axis=1), "seg")
        block = jnp.concatenate(
            [lax.dynamic_slice_in_dim(block[:, : window.shape[1]], per * mine_at, rows, axis=1),
             block[:, window.shape[1] :]],
            axis=1,
        )
    segs = block.shape[0]
    cos, sin = make_forward(length)
    flat_rows = block.reshape(segs * block.shape[1], length)
    spectra = jnp.concatenate(
        [
            jnp.dot(flat_rows, cos, preferred_element_type=jnp.float32),
            -jnp.dot(flat_rows, sin, preferred_element_type=jnp.float32),
        ],
        axis=-1,
    )
    white = whiten(spectra.reshape(block.shape), BAND).astype(jnp.bfloat16)
    chosen = white[:, rows:].reshape(segs, steps, nsrc, length)
    part = white[:, :rows]
    total = part[:, 0:per].astype(jnp.float32)
    for offset in range(1, LOW + HIGH + 1):
        total = total + part[:, offset : offset + per].astype(jnp.float32)
    stacked = (total * 0.125).astype(jnp.bfloat16)
    cross = cross_sum(stacked, chosen)
    flat = inverse_transform(cross.reshape(-1, length), LAGS)
    return flat.reshape(steps, nsrc, per, LAGS)


def solution(mesh):
    return jax.shard_map(
        shards,
        mesh=mesh,
        in_specs=(P("seg", "fibre", None), P(), P()),
        out_specs=P(None, None, ("fibre", "seg"), None),
        check_vma=False,
    )
```

```python
import math

import jax
import jax.numpy as jnp
from jax import lax
from jax.sharding import PartitionSpec as P

BAND = 128
LAGS = 1024
LOW = 4
HIGH = 3


def broadcast(block, axis, rider):
    count = lax.axis_size(axis)
    width = block.shape[1]
    both = lax.ppermute(jnp.concatenate([block, rider], axis=1), axis, [(i, i ^ 1) for i in range(count)])
    block = block + both[:, :width]
    carried = both[:, width:]
    strides = [1 << bit for bit in range(1, count.bit_length() - 1)]
    if count == 128:
        strides = [8, 4, 2, 16, 32, 64]
    for stride in strides:
        block = block + lax.ppermute(block, axis, [(i, i ^ stride) for i in range(count)])
    return block, carried


def gather(block, axis):
    count = lax.axis_size(axis)
    stride = count // 2
    while stride >= 1:
        partner = lax.ppermute(block, axis, [(i, i ^ stride) for i in range(count)])
        block = jnp.concatenate([block, partner], axis=0)
        stride //= 2
    return block


def edges(cells, axis):
    count = lax.axis_size(axis)
    odd = lax.axis_index(axis) % 2 == 1
    perm = [(i, i + 1) if i % 2 else (i, i - 1) for i in range(count)]
    perm = [(i, j) for i, j in perm if 0 <= j < count]
    return cells, lax.ppermute(cells, axis, perm), odd


def halo(cells, near, far, odd):
    rows = cells.shape[1]
    lower = jnp.where(odd, near[:, rows - LOW :], far[:, rows - LOW :])
    upper = jnp.where(odd, far[:, :HIGH], near[:, :HIGH])
    return jnp.concatenate([lower, cells, upper], axis=1)


def cos_sin(phase, period):
    angle = phase.astype(jnp.float32) * (2.0 * math.pi / period)
    return jnp.cos(angle), jnp.sin(angle)


def make_forward(length):
    half = length // 2
    lo_count = 64
    hi_count = length // lo_count
    freqs = jnp.arange(half, dtype=jnp.int32)
    hi = jnp.arange(hi_count, dtype=jnp.int32)
    lo = jnp.arange(lo_count, dtype=jnp.int32)
    hi_c, hi_s = cos_sin(hi[:, None] * freqs[None, :] % hi_count, hi_count)
    lo_c, lo_s = cos_sin(lo[:, None] * freqs[None, :] % length, length)
    cos = hi_c[:, None, :] * lo_c[None, :, :] - hi_s[:, None, :] * lo_s[None, :, :]
    sin = hi_s[:, None, :] * lo_c[None, :, :] + hi_c[:, None, :] * lo_s[None, :, :]
    cos = cos.reshape(length, half).astype(jnp.bfloat16)
    sin = sin.reshape(length, half).astype(jnp.bfloat16)
    return cos, sin


def inverse_transform(cross, lags):
    count, length = cross.shape
    half = length // 2
    inner = 32
    outer = half // inner
    period = length // inner
    turns = lags // period
    shift = length - lags // 2
    hi = jnp.arange(outer, dtype=jnp.int32)
    lo = jnp.arange(inner, dtype=jnp.int32)
    cols = jnp.arange(period, dtype=jnp.int32)
    laps = jnp.arange(turns, dtype=jnp.int32)
    e_c, e_s = cos_sin(hi[:, None] * cols[None, :] % period, period)
    first = jnp.concatenate(
        [jnp.concatenate([e_c, e_s], axis=1), jnp.concatenate([-e_s, e_c], axis=1)], axis=0
    )
    parts = jnp.concatenate(
        [cross[:, :half].reshape(count, outer, inner), cross[:, half:].reshape(count, outer, inner)],
        axis=1,
    )
    spun = jnp.einsum("rab,am->rbm", parts, first, precision=lax.Precision.HIGHEST)
    u_re, u_im = spun[..., :period], spun[..., period:]
    t_c, t_s = cos_sin(lo[:, None] * (cols[None, :] + shift) % length, length)
    twisted = jnp.concatenate([u_re * t_c - u_im * t_s, u_re * t_s + u_im * t_c], axis=1)
    f_c, f_s = cos_sin(lo[:, None] * laps[None, :] % inner, inner)
    second = jnp.concatenate([f_c, -f_s], axis=0)
    out = jnp.einsum("rbm,bq->rqm", twisted, second, precision=lax.Precision.HIGHEST)
    return out.reshape(count, lags) * (1.0 / math.sqrt(half))


def whiten(spectra, band):
    lead = spectra.shape[:-1]
    width = spectra.shape[-1] // 2
    parts = spectra.reshape(lead + (2, width // band, band))
    power = jnp.sum(parts * parts, axis=(-3, -1)) / (2.0 * band)
    scale = lax.rsqrt(power + 1e-06)
    return (parts * scale[..., None, :, None]).reshape(spectra.shape)


def cross_sum(receivers, emitters):
    half = receivers.shape[-1] // 2
    rec = receivers.astype(jnp.float32)[:, None, None]
    emi = emitters.astype(jnp.float32)[:, :, :, None]
    rec_re, rec_im = (rec[..., :half], rec[..., half:])
    emi_re, emi_im = (emi[..., :half], emi[..., half:])
    real_part = jnp.sum(rec_re * emi_re, axis=0) + jnp.sum(rec_im * emi_im, axis=0)
    imag_part = jnp.sum(rec_im * emi_re, axis=0) - jnp.sum(rec_re * emi_im, axis=0)
    return jnp.concatenate([real_part, imag_part], axis=-1)


def shards(data, sources, owners):
    seg_dev, ch_dev, length = data.shape
    steps, nsrc = sources.shape
    seg_count = lax.axis_size("seg")
    per = ch_dev // seg_count
    here = lax.axis_index("fibre")
    channels = jnp.arange(ch_dev, dtype=jnp.int32)
    keep = (sources[:, :, None] == channels[None, None, :]) & (here == owners)[:, None, None]
    picked = jnp.sum(
        jnp.where(keep.reshape(1, steps * nsrc, ch_dev, 1), data[:, None], jnp.zeros_like(data[:, None])),
        axis=2,
    )
    rider, far, odd = edges(data, "fibre")
    received, near = broadcast(picked, "fibre", rider)
    window = halo(data, near, far, odd)
    rows = window.shape[1]
    block = jnp.concatenate([window, received], axis=1)
    block = gather(block, "seg")
    segs = block.shape[0]
    cos, sin = make_forward(length)
    flat_rows = block.reshape(segs * block.shape[1], length)
    spectra = jnp.concatenate(
        [
            jnp.dot(flat_rows, cos, preferred_element_type=jnp.float32),
            -jnp.dot(flat_rows, sin, preferred_element_type=jnp.float32),
        ],
        axis=-1,
    )
    white = whiten(spectra.reshape(block.shape), BAND).astype(jnp.bfloat16)
    chosen = white[:, rows:].reshape(segs, steps, nsrc, length)
    start = lax.axis_index("seg") * per
    part = lax.dynamic_slice_in_dim(white[:, :rows], start, per + LOW + HIGH, axis=1)
    total = part[:, 0:per].astype(jnp.float32)
    for offset in range(1, LOW + HIGH + 1):
        total = total + part[:, offset : offset + per].astype(jnp.float32)
    stacked = (total * 0.125).astype(jnp.bfloat16)
    cross = cross_sum(stacked, chosen)
    flat = inverse_transform(cross.reshape(-1, length), LAGS)
    return flat.reshape(steps, nsrc, per, LAGS)


def solution(mesh):
    return jax.shard_map(
        shards,
        mesh=mesh,
        in_specs=(P("seg", "fibre", None), P(), P()),
        out_specs=P(None, None, ("fibre", "seg"), None),
        check_vma=False,
    )
```
